256 devices in a mesh: wide: 64 (over x, z, core), narrow: 4 (over y).
Axes of the slice: x: 4, y: 4, z: 8, core: 2. Of those that a mesh axis runs over, the one named last changes fastest.
Arguments:
- attn_heads: bfloat16 [8192, 1536], P('wide', 'narrow'), may hold values from -6 to 6
- w_out: bfloat16 [1536, 1536], P('narrow'), may hold values from -0.21875 to 0.21875
- residual: bfloat16 [8192, 1536], P('wide', 'narrow'), may hold values from -6 to 6
- norm_gain: float32 [1536], replicated, may hold values from 0.1 to 1.9
- route_ids: int32 [8192, 4], P('wide'), may hold values from 0 to 31, all different within a row; in each aligned block of 128 rows (0 to 127, 128 to 255, ...) at most 32 rows name the same one
- route_weight: float32 [8192, 4], P('wide'), may hold values from 0.1 to 1
- row_order: int32 [8192], P('wide'), may hold values from 0 to 8191, as said below
- slot_expert: int32 [64], replicated, may hold values from 0 to 31, as said below
- w_in: bfloat16 [64, 2, 768, 1536], P('wide', None, 'narrow')
- w_down: bfloat16 [64, 768, 1536], P('wide', 'narrow')
Outputs:
- block_out: bfloat16 [8192, 1536], P('wide', 'narrow')
The draws below stay inside these ranges and needn't reach their ends.
Inputs may be any that keep to these rules, and one draw needn't show every extreme that they name: `route_ids`: each row names 4 different experts; among the 128 rows of one index of wide no expert is named more than 32 times. `row_order`: A permutation of the rows; of the 128 rows of each index of wide, exactly 2 have their initial position among the rows of each index of wide. `slot_expert`: every expert is held by one or more slots; slots holding the same expert hold equal w_in and w_down.
All inputs are finite; a program needn't handle non-finite values.
Results may differ from the reference program's by a relative error of at most 0.017.
Values may be sent and summed in bfloat16 or wider, within the bound.
No kernel may reach another device: no remote copies, remote signals or barrier semaphores. Data moves between devices by JAX's collectives and lax.ppermute only.
A program may use at most 128 MiB of HBM per device.

```python
import math
import jax
import jax.numpy as jnp
import numpy as np
from jax import lax

D = 1536
HID = 768
EXPERTS = 32
TOP = 4
TOK_DEV = 128
F = 1536
TOKENS = 8192
CAP = 32
SLOTS = 64
N_WIDE = 64
N_NARROW = 4


def slot_table(key):
    first = jax.random.permutation(jax.random.fold_in(key, 11), EXPERTS).astype(jnp.int32)
    extra = jax.random.randint(jax.random.fold_in(key, 12), (SLOTS - EXPERTS,), 0, EXPERTS).astype(jnp.int32)
    joined = jnp.concatenate([first, extra])
    return jax.random.permutation(jax.random.fold_in(key, 13), joined).astype(jnp.int32)


def draw_slot_expert(key, part):
    return slot_table(key)


def draw_w_in(key, part):
    table = slot_table(key)
    inner = jax.random.fold_in(key, 21)
    values = jax.random.normal(inner, (EXPERTS, 2, HID, D), jnp.float32)
    return (values * D ** (-0.5))[table].astype(jnp.bfloat16)


def draw_w_down(key, part):
    table = slot_table(key)
    inner = jax.random.fold_in(key, 22)
    values = jax.random.normal(inner, (EXPERTS, HID, D), jnp.float32)
    return (values * HID ** (-0.5))[table].astype(jnp.bfloat16)


def draw_row_order(key, part):
    blocks = TOKENS // TOK_DEV
    pair_rows = TOK_DEV // blocks
    source_keys = jax.random.split(jax.random.fold_in(key, 31), blocks)
    target_keys = jax.random.split(jax.random.fold_in(key, 32), blocks)
    source_perm = jax.vmap(lambda k: jax.random.permutation(k, TOK_DEV))(source_keys).astype(jnp.int32)
    target_perm = jax.vmap(lambda k: jax.random.permutation(k, TOK_DEV))(target_keys).astype(jnp.int32)
    src_index = jnp.arange(blocks, dtype=jnp.int32)[:, None, None]
    dst_index = jnp.arange(blocks, dtype=jnp.int32)[None, :, None]
    pair_index = jnp.arange(pair_rows, dtype=jnp.int32)[None, None, :]
    processed = src_index * TOK_DEV + source_perm[src_index, dst_index * pair_rows + pair_index]
    initial = dst_index * TOK_DEV + target_perm[dst_index, src_index * pair_rows + pair_index]
    return jnp.zeros((TOKENS,), jnp.int32).at[processed.reshape(-1)].set(initial.reshape(-1))


def with_spikes(entries, key, source, target, parts, factor):
    def block_of(dim):
        return (jnp.arange(entries.shape[dim]) // (entries.shape[dim] // parts)).reshape((-1,) + (1,) * (entries.ndim - 1 - dim))

    one_side = jax.random.permutation(key, parts)[block_of(target)]
    other_side = (block_of(target) + parts // 2) % parts
    return jnp.where((block_of(source) == one_side) | (block_of(source) == other_side), factor * entries, entries)


def block_scale(own_key, extent, shards, smallest, largest):
    def one(position, blocks):
        heights = jax.random.uniform(jax.random.fold_in(jax.random.fold_in(own_key, 6), position), (blocks,), jnp.float32, smallest / len(shards), largest / len(shards))
        return jnp.repeat(jnp.exp(heights), extent[position] // blocks).reshape((-1,) + (1,) * (len(extent) - position - 1))

    level = one(*shards[0])
    for cut in shards[1:]:
        level = level * one(*cut)
    return level


def assign_block(key, own, number, rows, amount, top, reach, lean):
    ranking = jax.random.permutation(key, amount)
    crowded, ordinary = shares(amount, rows * top, reach, lean, True), shares(amount, rows * top, reach, lean, False)
    places = jnp.arange(amount)

    def named(sizes, turn):
        used = int((sizes > 0).sum())
        fixed = max(1, used // 4)
        shifted = fixed + (places - fixed + turn * (used - fixed)) % max(1, amount - fixed)
        return jnp.zeros((amount,), jnp.int32).at[ranking[jnp.where(places < fixed, places, shifted)]].set(jnp.asarray(sizes, jnp.int32))

    sizes = jnp.where(number % 4 == 0, named(crowded, number // 4), named(ordinary, number - number // 4 - 1))
    mixed = jax.random.permutation(jax.random.fold_in(own, 3), amount)
    source_of, sink = mixed[0:amount // 2 * 2:2], mixed[1:amount // 2 * 2:2]
    margin = jnp.minimum(sizes[source_of] - 1, reach - sizes[sink]) // 2
    margin = jnp.where((source_of == ranking[0]) | (sink == ranking[0]) | (sizes[sink] == 0), 0, jnp.maximum(margin, 0))
    shifted = jax.random.randint(jax.random.fold_in(own, 4), (amount // 2,), 0, 1 << 20) % (margin + 1)
    sizes = sizes.at[source_of].add(-shifted).at[sink].add(shifted)
    members = jnp.searchsorted(jnp.cumsum(sizes), jnp.arange(rows * top), side="right").astype(jnp.int32)
    table = members.reshape(top, rows).T
    table = table[jax.random.permutation(jax.random.fold_in(own, 1), rows)]
    turn = jax.random.randint(jax.random.fold_in(own, 2), (rows, 1), 0, top)
    return jnp.take_along_axis(table, (jnp.arange(top)[None, :] + turn) % top, axis=1)


def shares(amount, total, reach, lean, full):
    loads = [(1 << 20) // math.isqrt(grade ** lean) + 1 for grade in range(1, amount + 1)]
    largest = reach if full else min(reach, max(-(-total // amount), total * loads[0] // sum(loads)))
    least = 1 if total - largest >= amount - 1 else 0
    counts, surplus = [largest] + [least] * (amount - 1), total - largest - least * (amount - 1)
    while surplus > 0:
        movable = [i for i in range(1, amount) if counts[i] < largest] or [i for i in range(1, amount) if counts[i] < reach]
        whole, remaining = sum([loads[i] for i in movable]), surplus
        for i in movable:
            more = min(reach - counts[i], max(1, remaining * loads[i] // whole), surplus)
            counts[i] = counts[i] + more
            surplus = surplus - more
    return np.array(counts)


def gaussian(stream_key, shape, spread, bound, cuts=(), held_as=jnp.bfloat16):
    level = block_scale(stream_key, shape, cuts, -0.22, 0.18) if cuts else 1.0
    array = jax.random.normal(stream_key, shape, jnp.float32) * spread * level
    return jnp.minimum(jnp.maximum(array, -bound), bound).astype(held_as)


def gaussian_with(rng, extent, scale, limit, cuts, heavy, kind=jnp.bfloat16):
    values = scale * jax.random.normal(rng, extent, jnp.float32)
    if cuts:
        values = values * block_scale(rng, extent, cuts, -0.22, 0.18)
    return jnp.clip(with_spikes(values, jax.random.fold_in(rng, 3), *heavy), -limit, limit).astype(kind)


def setup_inputs(seed: int = 0) -> dict:
    key_of = jax.random.split(jax.random.key(seed), 11)
    attn_heads = gaussian(key_of[0], (TOKENS, F), 1.0, 6.0, ((0, 64), (1, 4)))
    w_out = gaussian_with(key_of[1], (F, D), F ** -0.5, 0.21875, ((0, 4),), (0, 1, 4, 2.0))
    residual = gaussian(key_of[2], (TOKENS, D), 1.0, 6.0, ((0, 64), (1, 4)))
    norm_gain = jnp.clip(1.0 + 0.18 * jax.random.normal(key_of[3], (D,), jnp.float32), 0.1, 1.9)
    route_ids_keys = jax.random.split(jax.random.fold_in(key_of[4], 1), TOKENS // TOK_DEV)
    route_ids_turns = jax.random.permutation(jax.random.fold_in(key_of[4], 3), TOKENS // TOK_DEV)
    route_ids = jax.vmap(lambda own, number: assign_block(jax.random.fold_in(key_of[4], 2), own, number, TOK_DEV, EXPERTS, TOP, CAP, 2))(route_ids_keys, route_ids_turns).reshape((TOKENS, TOP))
    route_weight = jnp.clip(jnp.exp(math.log(1.0) - 2.3025851 * jax.random.uniform(key_of[5], (TOKENS, TOP), jnp.float32) ** block_scale(key_of[5], (TOKENS, TOP), ((0, 64),), -0.2, 0.2)), 0.1, 1.0)
    row_order = draw_row_order(jax.random.fold_in(key_of[10], 71), 0)
    slot_expert = draw_slot_expert(jax.random.fold_in(key_of[10], 71), 0)
    w_in = draw_w_in(jax.random.fold_in(key_of[10], 71), 0)
    w_down = draw_w_down(jax.random.fold_in(key_of[10], 71), 0)
    return {"attn_heads": attn_heads, "w_out": w_out, "residual": residual, "norm_gain": norm_gain, "route_ids": route_ids, "route_weight": route_weight, "row_order": row_order, "slot_expert": slot_expert, "w_in": w_in, "w_down": w_down}


def reference(attn_heads, w_out, residual, norm_gain, route_ids, route_weight, row_order, slot_expert, w_in, w_down):
    projected = jnp.dot(attn_heads, w_out, preferred_element_type=jnp.float32)
    hidden = (residual.astype(jnp.float32) + projected).astype(jnp.bfloat16)
    hidden_f = hidden.astype(jnp.float32)
    mean_sq = lax.optimization_barrier(jnp.mean(hidden_f * hidden_f, axis=1, keepdims=True))
    normed = (hidden_f * lax.rsqrt(mean_sq + 1e-06) * norm_gain).astype(jnp.bfloat16)
    flat_ids = route_ids.reshape(-1).astype(jnp.int32)
    total = flat_ids.shape[0]
    buffer_rows = N_WIDE * CAP
    quarter = HID // N_NARROW

    def one_expert(carry, expert):
        slot_index = jnp.argmax(slot_expert == expert).astype(jnp.int32)
        both = lax.dynamic_index_in_dim(w_in, slot_index, 0, keepdims=False)
        lower = lax.dynamic_index_in_dim(w_down, slot_index, 0, keepdims=False)
        picked = jnp.nonzero(flat_ids == expert, size=buffer_rows, fill_value=total)[0].astype(jnp.int32)
        source_rows = jnp.minimum(picked, total - 1) // TOP
        rows_in = normed[source_rows]
        gate = jnp.dot(rows_in, both[0].T, preferred_element_type=jnp.float32)
        upper = jnp.dot(rows_in, both[1].T, preferred_element_type=jnp.float32)
        active = (jax.nn.relu(gate) * upper).astype(jnp.bfloat16)
        summed = jnp.zeros((buffer_rows, D), jnp.float32)
        for quarter_index in range(N_NARROW):
            lo_edge = quarter_index * quarter
            piece = jnp.dot(active[:, lo_edge:lo_edge + quarter], lower[lo_edge:lo_edge + quarter], preferred_element_type=jnp.float32)
            summed = summed + lax.optimization_barrier(piece.astype(jnp.bfloat16)).astype(jnp.float32)
        carry = carry.at[picked].set(summed.astype(jnp.bfloat16), mode='drop')
        return (carry, None)
    expert_out, _ = lax.scan(one_expert, jnp.zeros((total, D), jnp.bfloat16), jnp.arange(EXPERTS, dtype=jnp.int32))
    weighted = route_weight[:, :, None] * expert_out.reshape(TOKENS, TOP, D).astype(jnp.float32)
    mixed = (hidden_f + lax.optimization_barrier(jnp.sum(weighted, axis=1))).astype(jnp.bfloat16)
    return jnp.zeros_like(mixed).at[row_order].set(mixed)
```

```python
import jax
import jax.numpy as jnp
from jax import lax
from jax.sharding import PartitionSpec as P

EXPERTS = 32
CAP = 32


def running_rank(onehot):
    return jnp.sum((jnp.cumsum(onehot, axis=0) - onehot) * onehot, axis=1)


def local(
    attn_heads,
    w_out,
    residual,
    norm_gain,
    route_ids,
    route_weight,
    row_order,
    slot_expert,
    w_in,
    w_down,
):
    row_count = residual.shape[0]
    wide_count = lax.axis_size("wide")
    narrow_count = lax.axis_size("narrow")
    width_local = residual.shape[1]
    model_width = width_local * narrow_count
    me_narrow = lax.axis_index("narrow")

    slot_local = w_in.shape[0]
    hid_local = w_down.shape[1]
    wd = w_down.reshape(slot_local, hid_local, narrow_count, width_local)
    wd = jnp.moveaxis(wd, 2, 0)
    wd_cols = lax.all_to_all(wd, "narrow", split_axis=0, concat_axis=0, tiled=True)

    partial_terms = jnp.dot(attn_heads, w_out, preferred_element_type=jnp.float32)
    projected = lax.psum_scatter(
        partial_terms.astype(jnp.bfloat16), "narrow", scatter_dimension=1, tiled=True
    ).astype(jnp.float32)
    hidden = (residual.astype(jnp.float32) + projected).astype(jnp.bfloat16)
    hidden_f = hidden.astype(jnp.float32)
    sum_sq = lax.psum(jnp.sum(hidden_f * hidden_f, axis=1, keepdims=True), "narrow")
    mean_sq = sum_sq / model_width
    gain_local = lax.dynamic_slice_in_dim(norm_gain, me_narrow * width_local, width_local)
    normed = (hidden_f * lax.rsqrt(mean_sq + 1e-06) * gain_local).astype(jnp.bfloat16)

    slot_count = slot_expert.shape[0]
    top_count = route_ids.shape[1]
    held = (slot_expert[None, :] == jnp.arange(EXPERTS, dtype=jnp.int32)[:, None]).astype(jnp.int32)
    copies = jnp.sum(held, axis=1)
    replica_rank = jnp.cumsum(held, axis=1) - held
    flat_ids = route_ids.reshape(-1)
    choose_expert = (flat_ids[:, None] == jnp.arange(EXPERTS, dtype=jnp.int32)[None, :]).astype(
        jnp.int32
    )
    copy_count = jnp.sum(choose_expert * copies[None, :], axis=1)
    replica = jnp.repeat(row_order, top_count) % copy_count
    held_rows = jnp.sum(choose_expert[:, :, None] * held[None, :, :], axis=1)
    rank_rows = jnp.sum(choose_expert[:, :, None] * replica_rank[None, :, :], axis=1)
    slot_hit = held_rows * (rank_rows == replica[:, None]).astype(jnp.int32)
    slot_index = jnp.sum(slot_hit * jnp.arange(slot_count, dtype=jnp.int32)[None, :], axis=1)
    position = slot_index * CAP + running_rank(slot_hit)
    outgoing = (
        jnp.zeros((slot_count * CAP, width_local), jnp.bfloat16)
        .at[position]
        .set(jnp.repeat(normed, top_count, axis=0))
    )
    outgoing = outgoing.reshape(wide_count, slot_local, CAP, width_local)
    arrived = lax.all_to_all(outgoing, "wide", split_axis=0, concat_axis=0, tiled=True)
    whole = lax.all_gather(arrived, "narrow", axis=0, tiled=False)
    w_in_q = w_in.reshape(slot_local, 2, hid_local, narrow_count, width_local)
    gate_up = jnp.einsum(
        "pnscd,sghpd->nscgh", whole, w_in_q, preferred_element_type=jnp.float32
    )
    active = (jax.nn.relu(gate_up[:, :, :, 0, :]) * gate_up[:, :, :, 1, :]).astype(jnp.bfloat16)
    active_all = lax.all_gather(active, "narrow", axis=0, tiled=False)
    lowered = jnp.einsum(
        "qnsch,qshd->qnscd", active_all, wd_cols, preferred_element_type=jnp.float32
    )
    pieces = lowered.astype(jnp.bfloat16).astype(jnp.float32)
    summed = jnp.sum(pieces, axis=0).astype(jnp.bfloat16)
    returned = lax.all_to_all(summed, "wide", split_axis=0, concat_axis=0, tiled=True)
    expert_out = returned.reshape(slot_count * CAP, width_local)[position]
    weighted = route_weight[:, :, None] * expert_out.reshape(
        row_count, top_count, width_local
    ).astype(jnp.float32)
    mixed = (hidden_f + jnp.sum(weighted, axis=1)).astype(jnp.bfloat16)
    pair_rows = row_count // wide_count
    target_dev = row_order // row_count
    target_place = row_order % row_count
    choose_target = (
        target_dev[:, None] == jnp.arange(wide_count, dtype=jnp.int32)[None, :]
    ).astype(jnp.int32)
    packed_index = target_dev * pair_rows + running_rank(choose_target)
    packed = jnp.zeros((row_count, width_local), jnp.bfloat16).at[packed_index].set(mixed)
    places = jnp.zeros((row_count,), jnp.int32).at[packed_index].set(target_place)
    arrived_rows, arrived_places = (
        lax.all_to_all(
            packed.reshape(wide_count, pair_rows, width_local),
            "wide",
            split_axis=0,
            concat_axis=0,
            tiled=True,
        ),
        lax.all_to_all(
            places.reshape(wide_count, pair_rows), "wide", split_axis=0, concat_axis=0, tiled=True
        ),
    )
    return (
        jnp.zeros((row_count, width_local), jnp.bfloat16)
        .at[arrived_places.reshape(-1)]
        .set(arrived_rows.reshape(row_count, width_local))
    )


def solution(mesh):
    placed = (
        P("wide", "narrow"),
        P("narrow", None),
        P("wide", "narrow"),
        P(),
        P("wide", None),
        P("wide", None),
        P("wide"),
        P(),
        P("wide", None, "narrow", None),
        P("wide", "narrow", None),
    )
    return jax.shard_map(
        local, mesh=mesh, in_specs=placed, out_specs=P("wide", "narrow"), check_vma=False
    )
```

```python
import jax
import jax.numpy as jnp
from jax import lax
from jax.sharding import PartitionSpec as P

EXPERTS = 32
CAP = 32


def running_rank(onehot):
    return jnp.sum((jnp.cumsum(onehot, axis=0) - onehot) * onehot, axis=1)


def local(
    attn_heads,
    w_out,
    residual,
    norm_gain,
    route_ids,
    route_weight,
    row_order,
    slot_expert,
    w_in,
    w_down,
):
    row_count = residual.shape[0]
    wide_count = lax.axis_size("wide")
    narrow_count = lax.axis_size("narrow")
    width_local = residual.shape[1]
    model_width = width_local * narrow_count
    me_narrow = lax.axis_index("narrow")

    slot_local = w_in.shape[0]
    w_in_all = lax.all_gather(w_in, "narrow", axis=0, tiled=False)
    w_down_all = lax.all_gather(w_down, "narrow", axis=0, tiled=False)

    partial_terms = jnp.dot(attn_heads, w_out, preferred_element_type=jnp.float32)
    projected = lax.psum_scatter(
        partial_terms.astype(jnp.bfloat16), "narrow", scatter_dimension=1, tiled=True
    ).astype(jnp.float32)
    hidden = (residual.astype(jnp.float32) + projected).astype(jnp.bfloat16)
    hidden_f = hidden.astype(jnp.float32)
    whole_rows = lax.all_gather(hidden, "narrow", axis=1, tiled=True).astype(jnp.float32)
    mean_sq = jnp.mean(whole_rows * whole_rows, axis=1, keepdims=True)
    normed = (whole_rows * lax.rsqrt(mean_sq + 1e-06) * norm_gain).astype(jnp.bfloat16)

    slot_count = slot_expert.shape[0]
    top_count = route_ids.shape[1]
    band = CAP // narrow_count
    held = (slot_expert[None, :] == jnp.arange(EXPERTS, dtype=jnp.int32)[:, None]).astype(jnp.int32)
    copies = jnp.sum(held, axis=1)
    replica_rank = jnp.cumsum(held, axis=1) - held
    flat_ids = route_ids.reshape(-1)
    choose_expert = (flat_ids[:, None] == jnp.arange(EXPERTS, dtype=jnp.int32)[None, :]).astype(
        jnp.int32
    )
    copy_count = jnp.sum(choose_expert * copies[None, :], axis=1)
    replica = jnp.repeat(row_order, top_count) % copy_count
    held_rows = jnp.sum(choose_expert[:, :, None] * held[None, :, :], axis=1)
    rank_rows = jnp.sum(choose_expert[:, :, None] * replica_rank[None, :, :], axis=1)
    slot_hit = held_rows * (rank_rows == replica[:, None]).astype(jnp.int32)
    slot_index = jnp.sum(slot_hit * jnp.arange(slot_count, dtype=jnp.int32)[None, :], axis=1)
    rank = running_rank(slot_hit)
    position = slot_index * CAP + rank
    send_at = jnp.where(
        rank // band == me_narrow, slot_index * band + rank % band, slot_count * band
    )
    outgoing = (
        jnp.zeros((slot_count * band, model_width), jnp.bfloat16)
        .at[send_at]
        .set(jnp.repeat(normed, top_count, axis=0), mode="drop")
    )
    outgoing = outgoing.reshape(wide_count, slot_local, band, model_width)
    arrived = lax.all_to_all(outgoing, "wide", split_axis=0, concat_axis=0, tiled=True)
    gate_up = jnp.einsum(
        "nscd,qsghd->nscgqh", arrived, w_in_all, preferred_element_type=jnp.float32
    )
    active = (jax.nn.relu(gate_up[:, :, :, 0]) * gate_up[:, :, :, 1]).astype(jnp.bfloat16)
    lowered = jnp.einsum(
        "nscqh,qshd->qnscd", active, w_down_all, preferred_element_type=jnp.float32
    )
    pieces = lowered.astype(jnp.bfloat16).astype(jnp.float32)
    summed = jnp.sum(pieces, axis=0).astype(jnp.bfloat16)
    summed = summed.reshape(wide_count, slot_local, band, narrow_count, width_local)
    summed = lax.all_to_all(summed, "narrow", split_axis=3, concat_axis=2, tiled=True)
    summed = summed.reshape(wide_count, slot_local, CAP, width_local)
    returned = lax.all_to_all(summed, "wide", split_axis=0, concat_axis=0, tiled=True)
    expert_out = returned.reshape(slot_count * CAP, width_local)[position]
    weighted = route_weight[:, :, None] * expert_out.reshape(
        row_count, top_count, width_local
    ).astype(jnp.float32)
    mixed = (hidden_f + jnp.sum(weighted, axis=1)).astype(jnp.bfloat16)
    pair_rows = row_count // wide_count
    target_dev = row_order // row_count
    target_place = row_order % row_count
    choose_target = (
        target_dev[:, None] == jnp.arange(wide_count, dtype=jnp.int32)[None, :]
    ).astype(jnp.int32)
    packed_index = target_dev * pair_rows + running_rank(choose_target)
    packed = jnp.zeros((row_count, width_local), jnp.bfloat16).at[packed_index].set(mixed)
    places = jnp.zeros((row_count,), jnp.int32).at[packed_index].set(target_place)
    arrived_rows, arrived_places = (
        lax.all_to_all(
            packed.reshape(wide_count, pair_rows, width_local),
            "wide",
            split_axis=0,
            concat_axis=0,
            tiled=True,
        ),
        lax.all_to_all(
            places.reshape(wide_count, pair_rows), "wide", split_axis=0, concat_axis=0, tiled=True
        ),
    )
    return (
        jnp.zeros((row_count, width_local), jnp.bfloat16)
        .at[arrived_places.reshape(-1)]
        .set(arrived_rows.reshape(row_count, width_local))
    )


def solution(mesh):
    placed = (
        P("wide", "narrow"),
        P("narrow", None),
        P("wide", "narrow"),
        P(),
        P("wide", None),
        P("wide", None),
        P("wide"),
        P(),
        P("wide", None, "narrow", None),
        P("wide", "narrow", None),
    )
    return jax.shard_map(
        local, mesh=mesh, in_specs=placed, out_specs=P("wide", "narrow"), check_vma=False
    )
```

```python
import jax
import jax.numpy as jnp
from jax import lax
from jax.sharding import PartitionSpec as P

EXPERTS = 32
CAP = 32


def running_rank(onehot):
    return jnp.sum((jnp.cumsum(onehot, axis=0) - onehot) * onehot, axis=1)


def local(
    attn_heads,
    w_out,
    residual,
    norm_gain,
    route_ids,
    route_weight,
    row_order,
    slot_expert,
    w_in,
    w_down,
):
    row_count = residual.shape[0]
    wide_count = lax.axis_size("wide")
    narrow_count = lax.axis_size("narrow")
    width_local = residual.shape[1]
    model_width = width_local * narrow_count
    me_narrow = lax.axis_index("narrow")

    slot_local = w_in.shape[0]
    hid_local = w_down.shape[1]
    both = jnp.concatenate(
        [w_in.reshape(slot_local, 2 * hid_local, model_width), w_down], axis=1
    )
    both = lax.all_gather(both, "narrow", axis=0, tiled=False)
    w_in_all = both[:, :, : 2 * hid_local].reshape(
        narrow_count, slot_local, 2, hid_local, model_width
    )
    w_down_all = both[:, :, 2 * hid_local :]

    partial_terms = jnp.dot(attn_heads, w_out, preferred_element_type=jnp.float32)
    projected = lax.psum_scatter(
        partial_terms.astype(jnp.bfloat16), "narrow", scatter_dimension=1, tiled=True
    ).astype(jnp.float32)
    hidden = (residual.astype(jnp.float32) + projected).astype(jnp.bfloat16)
    hidden_f = hidden.astype(jnp.float32)
    whole_rows = lax.all_gather(hidden, "narrow", axis=1, tiled=True).astype(jnp.float32)
    mean_sq = jnp.mean(whole_rows * whole_rows, axis=1, keepdims=True)
    normed = (whole_rows * lax.rsqrt(mean_sq + 1e-06) * norm_gain).astype(jnp.bfloat16)

    slot_count = slot_expert.shape[0]
    top_count = route_ids.shape[1]
    band = CAP // narrow_count
    held = (slot_expert[None, :] == jnp.arange(EXPERTS, dtype=jnp.int32)[:, None]).astype(jnp.int32)
    copies = jnp.sum(held, axis=1)
    replica_rank = jnp.cumsum(held, axis=1) - held
    flat_ids = route_ids.reshape(-1)
    choose_expert = (flat_ids[:, None] == jnp.arange(EXPERTS, dtype=jnp.int32)[None, :]).astype(
        jnp.int32
    )
    copy_count = jnp.sum(choose_expert * copies[None, :], axis=1)
    replica = jnp.repeat(row_order, top_count) % copy_count
    held_rows = jnp.sum(choose_expert[:, :, None] * held[None, :, :], axis=1)
    rank_rows = jnp.sum(choose_expert[:, :, None] * replica_rank[None, :, :], axis=1)
    slot_hit = held_rows * (rank_rows == replica[:, None]).astype(jnp.int32)
    slot_index = jnp.sum(slot_hit * jnp.arange(slot_count, dtype=jnp.int32)[None, :], axis=1)
    rank = running_rank(slot_hit)
    position = slot_index * CAP + rank
    send_at = jnp.where(
        rank // band == me_narrow, slot_index * band + rank % band, slot_count * band
    )
    outgoing = (
        jnp.zeros((slot_count * band, model_width), jnp.bfloat16)
        .at[send_at]
        .set(jnp.repeat(normed, top_count, axis=0), mode="drop")
    )
    outgoing = outgoing.reshape(wide_count, slot_local, band, model_width)
    arrived = lax.all_to_all(outgoing, "wide", split_axis=0, concat_axis=0, tiled=True)
    gate_up = jnp.einsum(
        "nscd,qsghd->nscgqh", arrived, w_in_all, preferred_element_type=jnp.float32
    )
    active = (jax.nn.relu(gate_up[:, :, :, 0]) * gate_up[:, :, :, 1]).astype(jnp.bfloat16)
    lowered = jnp.einsum(
        "nscqh,qshd->qnscd", active, w_down_all, preferred_element_type=jnp.float32
    )
    pieces = lowered.astype(jnp.bfloat16).astype(jnp.float32)
    summed = jnp.sum(pieces, axis=0).astype(jnp.bfloat16)
    summed = summed.reshape(wide_count, slot_local, band, narrow_count, width_local)
    summed = lax.all_to_all(summed, "narrow", split_axis=3, concat_axis=2, tiled=True)
    summed = summed.reshape(wide_count, slot_local, CAP, width_local)
    returned = lax.all_to_all(summed, "wide", split_axis=0, concat_axis=0, tiled=True)
    expert_out = returned.reshape(slot_count * CAP, width_local)[position]
    weighted = route_weight[:, :, None] * expert_out.reshape(
        row_count, top_count, width_local
    ).astype(jnp.float32)
    mixed = (hidden_f + jnp.sum(weighted, axis=1)).astype(jnp.bfloat16)
    pair_rows = row_count // wide_count
    target_dev = row_order // row_count
    target_place = row_order % row_count
    choose_target = (
        target_dev[:, None] == jnp.arange(wide_count, dtype=jnp.int32)[None, :]
    ).astype(jnp.int32)
    packed_index = target_dev * pair_rows + running_rank(choose_target)
    packed = jnp.zeros((row_count, width_local), jnp.bfloat16).at[packed_index].set(mixed)
    places = jnp.zeros((row_count,), jnp.int32).at[packed_index].set(target_place)
    assert row_count <= 256 and pair_rows <= width_local
    place_row = jnp.zeros((wide_count, 1, width_local), jnp.bfloat16)
    place_row = place_row.at[:, 0, :pair_rows].set(
        places.reshape(wide_count, pair_rows).astype(jnp.bfloat16)
    )
    packed = jnp.concatenate(
        [packed.reshape(wide_count, pair_rows, width_local), place_row], axis=1
    )
    arrived_all = lax.all_to_all(packed, "wide", split_axis=0, concat_axis=0, tiled=True)
    arrived_rows = arrived_all[:, :pair_rows]
    arrived_places = arrived_all[:, pair_rows, :pair_rows].astype(jnp.int32)
    return (
        jnp.zeros((row_count, width_local), jnp.bfloat16)
        .at[arrived_places.reshape(-1)]
        .set(arrived_rows.reshape(row_count, width_local))
    )


def solution(mesh):
    placed = (
        P("wide", "narrow"),
        P("narrow", None),
        P("wide", "narrow"),
        P(),
        P("wide", None),
        P("wide", None),
        P("wide"),
        P(),
        P("wide", None, "narrow", None),
        P("wide", "narrow", None),
    )
    return jax.shard_map(
        local, mesh=mesh, in_specs=placed, out_specs=P("wide", "narrow"), check_vma=False
    )
```

```python
import jax
import jax.numpy as jnp
from jax import lax
from jax.sharding import PartitionSpec as P

EXPERTS = 32
CAP = 32


def running_rank(onehot):
    return jnp.sum((jnp.cumsum(onehot, axis=0) - onehot) * onehot, axis=1)


def local(
    attn_heads,
    w_out,
    residual,
    norm_gain,
    route_ids,
    route_weight,
    row_order,
    slot_expert,
    w_in,
    w_down,
):
    row_count = residual.shape[0]
    wide_count = lax.axis_size("wide")
    narrow_count = lax.axis_size("narrow")
    width_local = residual.shape[1]
    model_width = width_local * narrow_count
    me_narrow = lax.axis_index("narrow")

    slot_local = w_in.shape[0]
    hid_local = w_down.shape[1]
    w_in_all = lax.all_gather(w_in, "narrow", axis=0, tiled=False)
    w_down_all = lax.all_gather(w_down, "narrow", axis=0, tiled=False)

    partial_terms = jnp.dot(attn_heads, w_out, preferred_element_type=jnp.float32)
    projected = lax.psum_scatter(
        partial_terms.astype(jnp.bfloat16), "narrow", scatter_dimension=1, tiled=True
    ).astype(jnp.float32)
    hidden = (residual.astype(jnp.float32) + projected).astype(jnp.bfloat16)
    hidden_f = hidden.astype(jnp.float32)
    whole_rows = lax.all_gather(hidden, "narrow", axis=1, tiled=True).astype(jnp.float32)
    mean_sq = jnp.mean(whole_rows * whole_rows, axis=1, keepdims=True)
    normed = (whole_rows * lax.rsqrt(mean_sq + 1e-06) * norm_gain).astype(jnp.bfloat16)

    slot_count = slot_expert.shape[0]
    top_count = route_ids.shape[1]
    band = CAP // narrow_count
    held = (slot_expert[None, :] == jnp.arange(EXPERTS, dtype=jnp.int32)[:, None]).astype(jnp.int32)
    copies = jnp.sum(held, axis=1)
    replica_rank = jnp.cumsum(held, axis=1) - held
    flat_ids = route_ids.reshape(-1)
    choose_expert = (flat_ids[:, None] == jnp.arange(EXPERTS, dtype=jnp.int32)[None, :]).astype(
        jnp.int32
    )
    copy_count = jnp.sum(choose_expert * copies[None, :], axis=1)
    replica = jnp.repeat(row_order, top_count) % copy_count
    held_rows = jnp.sum(choose_expert[:, :, None] * held[None, :, :], axis=1)
    rank_rows = jnp.sum(choose_expert[:, :, None] * replica_rank[None, :, :], axis=1)
    slot_hit = held_rows * (rank_rows == replica[:, None]).astype(jnp.int32)
    slot_index = jnp.sum(slot_hit * jnp.arange(slot_count, dtype=jnp.int32)[None, :], axis=1)
    rank = running_rank(slot_hit)
    position = slot_index * CAP + rank
    send_at = jnp.where(
        rank // band == me_narrow, slot_index * band + rank % band, slot_count * band
    )
    outgoing = (
        jnp.zeros((slot_count * band, model_width), jnp.bfloat16)
        .at[send_at]
        .set(jnp.repeat(normed, top_count, axis=0), mode="drop")
    )
    outgoing = outgoing.reshape(wide_count, slot_local, band, model_width)
    arrived = lax.all_to_all(outgoing, "wide", split_axis=0, concat_axis=0, tiled=True)
    gate_up = jnp.einsum(
        "nscd,qsghd->nscgqh", arrived, w_in_all, preferred_element_type=jnp.float32
    )
    active = (jax.nn.relu(gate_up[:, :, :, 0]) * gate_up[:, :, :, 1]).astype(jnp.bfloat16)
    w_down_cols = w_down_all.reshape(
        narrow_count, slot_local, hid_local, narrow_count, width_local
    )
    lowered = jnp.einsum(
        "nscqh,qshpd->qnpscd", active, w_down_cols, preferred_element_type=jnp.float32
    )
    pieces = lowered.astype(jnp.bfloat16).astype(jnp.float32)
    summed = jnp.sum(pieces, axis=0).astype(jnp.bfloat16)
    summed = summed.reshape(wide_count * narrow_count, slot_local, band, width_local)
    returned = lax.all_to_all(
        summed, ("wide", "narrow"), split_axis=0, concat_axis=0, tiled=True
    )
    returned = returned.reshape(wide_count, narrow_count, slot_local, band, width_local)
    returned = jnp.swapaxes(returned, 1, 2)
    expert_out = returned.reshape(slot_count * CAP, width_local)[position]
    weighted = route_weight[:, :, None] * expert_out.reshape(
        row_count, top_count, width_local
    ).astype(jnp.float32)
    mixed = (hidden_f + jnp.sum(weighted, axis=1)).astype(jnp.bfloat16)
    pair_rows = row_count // wide_count
    target_dev = row_order // row_count
    target_place = row_order % row_count
    choose_target = (
        target_dev[:, None] == jnp.arange(wide_count, dtype=jnp.int32)[None, :]
    ).astype(jnp.int32)
    packed_index = target_dev * pair_rows + running_rank(choose_target)
    packed = jnp.zeros((row_count, width_local), jnp.bfloat16).at[packed_index].set(mixed)
    places = jnp.zeros((row_count,), jnp.int32).at[packed_index].set(target_place)
    assert row_count <= 256 and pair_rows <= width_local
    place_row = jnp.zeros((wide_count, 1, width_local), jnp.bfloat16)
    place_row = place_row.at[:, 0, :pair_rows].set(
        places.reshape(wide_count, pair_rows).astype(jnp.bfloat16)
    )
    packed = jnp.concatenate(
        [packed.reshape(wide_count, pair_rows, width_local), place_row], axis=1
    )
    arrived_all = lax.all_to_all(packed, "wide", split_axis=0, concat_axis=0, tiled=True)
    arrived_rows = arrived_all[:, :pair_rows]
    arrived_places = arrived_all[:, pair_rows, :pair_rows].astype(jnp.int32)
    return (
        jnp.zeros((row_count, width_local), jnp.bfloat16)
        .at[arrived_places.reshape(-1)]
        .set(arrived_rows.reshape(row_count, width_local))
    )


def solution(mesh):
    placed = (
        P("wide", "narrow"),
        P("narrow", None),
        P("wide", "narrow"),
        P(),
        P("wide", None),
        P("wide", None),
        P("wide"),
        P(),
        P("wide", None, "narrow", None),
        P("wide", "narrow", None),
    )
    return jax.shard_map(
        local, mesh=mesh, in_specs=placed, out_specs=P("wide", "narrow"), check_vma=False
    )
```

```python
import jax
import jax.numpy as jnp
from jax import lax
from jax.sharding import PartitionSpec as P

EXPERTS = 32
CAP = 32


def running_rank(onehot):
    return jnp.sum((jnp.cumsum(onehot, axis=0) - onehot) * onehot, axis=1)


def local(
    attn_heads,
    w_out,
    residual,
    norm_gain,
    route_ids,
    route_weight,
    row_order,
    slot_expert,
    w_in,
    w_down,
):
    row_count = residual.shape[0]
    wide_count = lax.axis_size("wide")
    narrow_count = lax.axis_size("narrow")
    width_local = residual.shape[1]
    model_width = width_local * narrow_count
    me_narrow = lax.axis_index("narrow")

    slot_local = w_in.shape[0]
    hid_local = w_down.shape[1]
    w_in_all = lax.all_gather(w_in, "narrow", axis=0, tiled=False)
    w_down_all = lax.all_gather(w_down, "narrow", axis=0, tiled=False)

    partial_terms = jnp.dot(attn_heads, w_out, preferred_element_type=jnp.float32)
    partial_terms = partial_terms.astype(jnp.bfloat16).reshape(
        row_count, narrow_count, width_local
    )
    partial_terms = jnp.swapaxes(partial_terms, 0, 1)
    partial_terms = lax.all_to_all(partial_terms, "narrow", split_axis=0, concat_axis=0, tiled=True)
    projected = jnp.sum(partial_terms.astype(jnp.float32), axis=0)
    hidden = (residual.astype(jnp.float32) + projected).astype(jnp.bfloat16)
    hidden_f = hidden.astype(jnp.float32)
    whole_rows = lax.all_gather(hidden, "narrow", axis=1, tiled=True).astype(jnp.float32)
    mean_sq = jnp.mean(whole_rows * whole_rows, axis=1, keepdims=True)
    normed = (whole_rows * lax.rsqrt(mean_sq + 1e-06) * norm_gain).astype(jnp.bfloat16)

    slot_count = slot_expert.shape[0]
    top_count = route_ids.shape[1]
    band = CAP // narrow_count
    held = (slot_expert[None, :] == jnp.arange(EXPERTS, dtype=jnp.int32)[:, None]).astype(jnp.int32)
    copies = jnp.sum(held, axis=1)
    replica_rank = jnp.cumsum(held, axis=1) - held
    flat_ids = route_ids.reshape(-1)
    choose_expert = (flat_ids[:, None] == jnp.arange(EXPERTS, dtype=jnp.int32)[None, :]).astype(
        jnp.int32
    )
    copy_count = jnp.sum(choose_expert * copies[None, :], axis=1)
    replica = jnp.repeat(row_order, top_count) % copy_count
    held_rows = jnp.sum(choose_expert[:, :, None] * held[None, :, :], axis=1)
    rank_rows = jnp.sum(choose_expert[:, :, None] * replica_rank[None, :, :], axis=1)
    slot_hit = held_rows * (rank_rows == replica[:, None]).astype(jnp.int32)
    slot_index = jnp.sum(slot_hit * jnp.arange(slot_count, dtype=jnp.int32)[None, :], axis=1)
    rank = running_rank(slot_hit)
    position = slot_index * CAP + rank
    send_at = jnp.where(
        rank // band == me_narrow, slot_index * band + rank % band, slot_count * band
    )
    outgoing = (
        jnp.zeros((slot_count * band, model_width), jnp.bfloat16)
        .at[send_at]
        .set(jnp.repeat(normed, top_count, axis=0), mode="drop")
    )
    outgoing = outgoing.reshape(wide_count, slot_local, band, model_width)
    arrived = lax.all_to_all(outgoing, "wide", split_axis=0, concat_axis=0, tiled=True)
    gate_up = jnp.einsum(
        "nscd,qsghd->nscgqh", arrived, w_in_all, preferred_element_type=jnp.float32
    )
    active = (jax.nn.relu(gate_up[:, :, :, 0]) * gate_up[:, :, :, 1]).astype(jnp.bfloat16)
    w_down_cols = w_down_all.reshape(
        narrow_count, slot_local, hid_local, narrow_count, width_local
    )
    lowered = jnp.einsum(
        "nscqh,qshpd->qnpscd", active, w_down_cols, preferred_element_type=jnp.float32
    )
    pieces = lowered.astype(jnp.bfloat16).astype(jnp.float32)
    summed = jnp.sum(pieces, axis=0).astype(jnp.bfloat16)
    summed = summed.reshape(wide_count * narrow_count, slot_local, band, width_local)
    returned = lax.all_to_all(
        summed, ("wide", "narrow"), split_axis=0, concat_axis=0, tiled=True
    )
    returned = returned.reshape(wide_count, narrow_count, slot_local, band, width_local)
    returned = jnp.swapaxes(returned, 1, 2)
    expert_out = returned.reshape(slot_count * CAP, width_local)[position]
    weighted = route_weight[:, :, None] * expert_out.reshape(
        row_count, top_count, width_local
    ).astype(jnp.float32)
    mixed = (hidden_f + jnp.sum(weighted, axis=1)).astype(jnp.bfloat16)
    pair_rows = row_count // wide_count
    target_dev = row_order // row_count
    target_place = row_order % row_count
    choose_target = (
        target_dev[:, None] == jnp.arange(wide_count, dtype=jnp.int32)[None, :]
    ).astype(jnp.int32)
    packed_index = target_dev * pair_rows + running_rank(choose_target)
    packed = jnp.zeros((row_count, width_local), jnp.bfloat16).at[packed_index].set(mixed)
    places = jnp.zeros((row_count,), jnp.int32).at[packed_index].set(target_place)
    assert row_count <= 256 and pair_rows <= width_local
    place_row = jnp.zeros((wide_count, 1, width_local), jnp.bfloat16)
    place_row = place_row.at[:, 0, :pair_rows].set(
        places.reshape(wide_count, pair_rows).astype(jnp.bfloat16)
    )
    packed = jnp.concatenate(
        [packed.reshape(wide_count, pair_rows, width_local), place_row], axis=1
    )
    arrived_all = lax.all_to_all(packed, "wide", split_axis=0, concat_axis=0, tiled=True)
    arrived_rows = arrived_all[:, :pair_rows]
    arrived_places = arrived_all[:, pair_rows, :pair_rows].astype(jnp.int32)
    return (
        jnp.zeros((row_count, width_local), jnp.bfloat16)
        .at[arrived_places.reshape(-1)]
        .set(arrived_rows.reshape(row_count, width_local))
    )


def solution(mesh):
    placed = (
        P("wide", "narrow"),
        P("narrow", None),
        P("wide", "narrow"),
        P(),
        P("wide", None),
        P("wide", None),
        P("wide"),
        P(),
        P("wide", None, "narrow", None),
        P("wide", "narrow", None),
    )
    return jax.shard_map(
        local, mesh=mesh, in_specs=placed, out_specs=P("wide", "narrow"), check_vma=False
    )
```

```python
import jax
import jax.numpy as jnp
from jax import lax
from jax.sharding import PartitionSpec as P

EXPERTS = 32
CAP = 32


def running_rank(onehot):
    return jnp.sum((jnp.cumsum(onehot, axis=0) - onehot) * onehot, axis=1)


def local(
    attn_heads,
    w_out,
    residual,
    norm_gain,
    route_ids,
    route_weight,
    row_order,
    slot_expert,
    w_in,
    w_down,
):
    row_count = residual.shape[0]
    wide_count = lax.axis_size("wide")
    narrow_count = lax.axis_size("narrow")
    width_local = residual.shape[1]
    model_width = width_local * narrow_count
    me_narrow = lax.axis_index("narrow")

    slot_local = w_in.shape[0]
    hid_local = w_down.shape[1]
    w_in_all = lax.all_gather(w_in, "narrow", axis=0, tiled=False)
    shifted = [w_down] + [
        lax.ppermute(
            w_down,
            "narrow",
            perm=[(i, (i + k) % narrow_count) for i in range(narrow_count)],
        )
        for k in range(1, narrow_count)
    ]
    from_shift = (me_narrow - jnp.arange(narrow_count, dtype=jnp.int32)) % narrow_count
    w_down_all = jnp.take(jnp.stack(shifted), from_shift, axis=0)

    partial_terms = jnp.dot(attn_heads, w_out, preferred_element_type=jnp.float32)
    partial_terms = partial_terms.astype(jnp.bfloat16).reshape(
        row_count, narrow_count, width_local
    )
    partial_terms = jnp.swapaxes(partial_terms, 0, 1)
    partial_terms = lax.all_to_all(partial_terms, "narrow", split_axis=0, concat_axis=0, tiled=True)
    projected = jnp.sum(partial_terms.astype(jnp.float32), axis=0)
    hidden = (residual.astype(jnp.float32) + projected).astype(jnp.bfloat16)
    hidden_f = hidden.astype(jnp.float32)
    spread = jnp.broadcast_to(hidden[None], (narrow_count, row_count, width_local))
    spread = lax.all_to_all(spread, "narrow", split_axis=0, concat_axis=0, tiled=True)
    whole_rows = jnp.moveaxis(spread, 0, 1).reshape(row_count, model_width)
    whole_rows = whole_rows.astype(jnp.float32)
    mean_sq = jnp.mean(whole_rows * whole_rows, axis=1, keepdims=True)
    normed = (whole_rows * lax.rsqrt(mean_sq + 1e-06) * norm_gain).astype(jnp.bfloat16)

    slot_count = slot_expert.shape[0]
    top_count = route_ids.shape[1]
    band = CAP // narrow_count
    held = (slot_expert[None, :] == jnp.arange(EXPERTS, dtype=jnp.int32)[:, None]).astype(jnp.int32)
    copies = jnp.sum(held, axis=1)
    replica_rank = jnp.cumsum(held, axis=1) - held
    flat_ids = route_ids.reshape(-1)
    choose_expert = (flat_ids[:, None] == jnp.arange(EXPERTS, dtype=jnp.int32)[None, :]).astype(
        jnp.int32
    )
    copy_count = jnp.sum(choose_expert * copies[None, :], axis=1)
    replica = jnp.repeat(row_order, top_count) % copy_count
    held_rows = jnp.sum(choose_expert[:, :, None] * held[None, :, :], axis=1)
    rank_rows = jnp.sum(choose_expert[:, :, None] * replica_rank[None, :, :], axis=1)
    slot_hit = held_rows * (rank_rows == replica[:, None]).astype(jnp.int32)
    slot_index = jnp.sum(slot_hit * jnp.arange(slot_count, dtype=jnp.int32)[None, :], axis=1)
    rank = running_rank(slot_hit)
    position = slot_index * CAP + rank
    send_at = jnp.where(
        rank // band == me_narrow, slot_index * band + rank % band, slot_count * band
    )
    outgoing = (
        jnp.zeros((slot_count * band, model_width), jnp.bfloat16)
        .at[send_at]
        .set(jnp.repeat(normed, top_count, axis=0), mode="drop")
    )
    outgoing = outgoing.reshape(wide_count, slot_local, band, model_width)
    arrived = lax.all_to_all(outgoing, "wide", split_axis=0, concat_axis=0, tiled=True)
    gate_up = jnp.einsum(
        "nscd,qsghd->nscgqh", arrived, w_in_all, preferred_element_type=jnp.float32
    )
    active = (jax.nn.relu(gate_up[:, :, :, 0]) * gate_up[:, :, :, 1]).astype(jnp.bfloat16)
    w_down_cols = w_down_all.reshape(
        narrow_count, slot_local, hid_local, narrow_count, width_local
    )
    lowered = jnp.einsum(
        "nscqh,qshpd->qnpscd", active, w_down_cols, preferred_element_type=jnp.float32
    )
    pieces = lowered.astype(jnp.bfloat16).astype(jnp.float32)
    summed = jnp.sum(pieces, axis=0).astype(jnp.bfloat16)
    summed = summed.reshape(wide_count * narrow_count, slot_local, band, width_local)
    returned = lax.all_to_all(
        summed, ("wide", "narrow"), split_axis=0, concat_axis=0, tiled=True
    )
    returned = returned.reshape(wide_count, narrow_count, slot_local, band, width_local)
    returned = jnp.swapaxes(returned, 1, 2)
    expert_out = returned.reshape(slot_count * CAP, width_local)[position]
    weighted = route_weight[:, :, None] * expert_out.reshape(
        row_count, top_count, width_local
    ).astype(jnp.float32)
    mixed = (hidden_f + jnp.sum(weighted, axis=1)).astype(jnp.bfloat16)
    pair_rows = row_count // wide_count
    target_dev = row_order // row_count
    target_place = row_order % row_count
    choose_target = (
        target_dev[:, None] == jnp.arange(wide_count, dtype=jnp.int32)[None, :]
    ).astype(jnp.int32)
    packed_index = target_dev * pair_rows + running_rank(choose_target)
    packed = jnp.zeros((row_count, width_local), jnp.bfloat16).at[packed_index].set(mixed)
    places = jnp.zeros((row_count,), jnp.int32).at[packed_index].set(target_place)
    assert row_count <= 256 and pair_rows <= width_local
    place_row = jnp.zeros((wide_count, 1, width_local), jnp.bfloat16)
    place_row = place_row.at[:, 0, :pair_rows].set(
        places.reshape(wide_count, pair_rows).astype(jnp.bfloat16)
    )
    packed = jnp.concatenate(
        [packed.reshape(wide_count, pair_rows, width_local), place_row], axis=1
    )
    arrived_all = lax.all_to_all(packed, "wide", split_axis=0, concat_axis=0, tiled=True)
    arrived_rows = arrived_all[:, :pair_rows]
    arrived_places = arrived_all[:, pair_rows, :pair_rows].astype(jnp.int32)
    return (
        jnp.zeros((row_count, width_local), jnp.bfloat16)
        .at[arrived_places.reshape(-1)]
        .set(arrived_rows.reshape(row_count, width_local))
    )


def solution(mesh):
    placed = (
        P("wide", "narrow"),
        P("narrow", None),
        P("wide", "narrow"),
        P(),
        P("wide", None),
        P("wide", None),
        P("wide"),
        P(),
        P("wide", None, "narrow", None),
        P("wide", "narrow", None),
    )
    return jax.shard_map(
        local, mesh=mesh, in_specs=placed, out_specs=P("wide", "narrow"), check_vma=False
    )
```

```python
import jax
import jax.numpy as jnp
from jax import lax
from jax.sharding import PartitionSpec as P

EXPERTS = 32
CAP = 32


def running_rank(onehot):
    return jnp.sum((jnp.cumsum(onehot, axis=0) - onehot) * onehot, axis=1)


def local(
    attn_heads,
    w_out,
    residual,
    norm_gain,
    route_ids,
    route_weight,
    row_order,
    slot_expert,
    w_in,
    w_down,
):
    row_count = residual.shape[0]
    wide_count = lax.axis_size("wide")
    narrow_count = lax.axis_size("narrow")
    width_local = residual.shape[1]
    model_width = width_local * narrow_count
    me_narrow = lax.axis_index("narrow")

    slot_local = w_in.shape[0]
    hid_local = w_down.shape[1]
    w_in_all = lax.all_gather(w_in, "narrow", axis=0, tiled=False)
    shifted = [w_down] + [
        lax.ppermute(
            w_down,
            "narrow",
            perm=[(i, (i + k) % narrow_count) for i in range(narrow_count)],
        )
        for k in range(1, narrow_count)
    ]
    from_shift = (me_narrow - jnp.arange(narrow_count, dtype=jnp.int32)) % narrow_count
    w_down_all = jnp.take(jnp.stack(shifted), from_shift, axis=0)

    partial_terms = jnp.dot(attn_heads, w_out, preferred_element_type=jnp.float32)
    partial_terms = partial_terms.astype(jnp.bfloat16).reshape(
        row_count, narrow_count, width_local
    )
    partial_terms = jnp.swapaxes(partial_terms, 0, 1)
    partial_terms = lax.all_to_all(partial_terms, "narrow", split_axis=0, concat_axis=0, tiled=True)
    projected = jnp.sum(partial_terms.astype(jnp.float32), axis=0)
    hidden = (residual.astype(jnp.float32) + projected).astype(jnp.bfloat16)
    hidden_f = hidden.astype(jnp.float32)
    spread = jnp.broadcast_to(hidden[None], (narrow_count, row_count, width_local))
    spread = lax.all_to_all(spread, "narrow", split_axis=0, concat_axis=0, tiled=True)
    whole_rows = jnp.moveaxis(spread, 0, 1).reshape(row_count, model_width)
    whole_rows = whole_rows.astype(jnp.float32)
    mean_sq = jnp.mean(whole_rows * whole_rows, axis=1, keepdims=True)
    normed = (whole_rows * lax.rsqrt(mean_sq + 1e-06) * norm_gain).astype(jnp.bfloat16)

    slot_count = slot_expert.shape[0]
    top_count = route_ids.shape[1]
    band = CAP // narrow_count
    held = (slot_expert[None, :] == jnp.arange(EXPERTS, dtype=jnp.int32)[:, None]).astype(jnp.int32)
    copies = jnp.sum(held, axis=1)
    replica_rank = jnp.cumsum(held, axis=1) - held
    flat_ids = route_ids.reshape(-1)
    choose_expert = (flat_ids[:, None] == jnp.arange(EXPERTS, dtype=jnp.int32)[None, :]).astype(
        jnp.int32
    )
    copy_count = jnp.sum(choose_expert * copies[None, :], axis=1)
    replica = jnp.repeat(row_order, top_count) % copy_count
    held_rows = jnp.sum(choose_expert[:, :, None] * held[None, :, :], axis=1)
    rank_rows = jnp.sum(choose_expert[:, :, None] * replica_rank[None, :, :], axis=1)
    slot_hit = held_rows * (rank_rows == replica[:, None]).astype(jnp.int32)
    slot_index = jnp.sum(slot_hit * jnp.arange(slot_count, dtype=jnp.int32)[None, :], axis=1)
    rank = running_rank(slot_hit)
    position = slot_index * CAP + rank
    send_at = jnp.where(
        rank // band == me_narrow, slot_index * band + rank % band, slot_count * band
    )
    picks = send_at.reshape(row_count, top_count)[None, :, :] == jnp.arange(
        slot_count * band, dtype=jnp.int32
    )[:, None, None]
    picks = jnp.any(picks, axis=2).astype(jnp.bfloat16)
    outgoing = jnp.dot(picks, normed, preferred_element_type=jnp.float32).astype(jnp.bfloat16)
    outgoing = outgoing.reshape(wide_count, slot_local, band, model_width)
    arrived = lax.all_to_all(outgoing, "wide", split_axis=0, concat_axis=0, tiled=True)
    gate_up = jnp.einsum(
        "nscd,qsghd->nscgqh", arrived, w_in_all, preferred_element_type=jnp.float32
    )
    active = (jax.nn.relu(gate_up[:, :, :, 0]) * gate_up[:, :, :, 1]).astype(jnp.bfloat16)
    w_down_cols = w_down_all.reshape(
        narrow_count, slot_local, hid_local, narrow_count, width_local
    )
    lowered = jnp.einsum(
        "nscqh,qshpd->qnpscd", active, w_down_cols, preferred_element_type=jnp.float32
    )
    pieces = lowered.astype(jnp.bfloat16).astype(jnp.float32)
    summed = jnp.sum(pieces, axis=0).astype(jnp.bfloat16)
    summed = summed.reshape(wide_count * narrow_count, slot_local, band, width_local)
    returned = lax.all_to_all(
        summed, ("wide", "narrow"), split_axis=0, concat_axis=0, tiled=True
    )
    returned = returned.reshape(wide_count, narrow_count, slot_local, band, width_local)
    returned = jnp.swapaxes(returned, 1, 2)
    expert_out = returned.reshape(slot_count * CAP, width_local)[position]
    weighted = route_weight[:, :, None] * expert_out.reshape(
        row_count, top_count, width_local
    ).astype(jnp.float32)
    mixed = (hidden_f + jnp.sum(weighted, axis=1)).astype(jnp.bfloat16)
    pair_rows = row_count // wide_count
    target_dev = row_order // row_count
    target_place = row_order % row_count
    choose_target = (
        target_dev[:, None] == jnp.arange(wide_count, dtype=jnp.int32)[None, :]
    ).astype(jnp.int32)
    packed_index = target_dev * pair_rows + running_rank(choose_target)
    packed = jnp.zeros((row_count, width_local), jnp.bfloat16).at[packed_index].set(mixed)
    places = jnp.zeros((row_count,), jnp.int32).at[packed_index].set(target_place)
    assert row_count <= 256 and pair_rows <= width_local
    place_row = jnp.zeros((wide_count, 1, width_local), jnp.bfloat16)
    place_row = place_row.at[:, 0, :pair_rows].set(
        places.reshape(wide_count, pair_rows).astype(jnp.bfloat16)
    )
    packed = jnp.concatenate(
        [packed.reshape(wide_count, pair_rows, width_local), place_row], axis=1
    )
    arrived_all = lax.all_to_all(packed, "wide", split_axis=0, concat_axis=0, tiled=True)
    arrived_rows = arrived_all[:, :pair_rows]
    arrived_places = arrived_all[:, pair_rows, :pair_rows].astype(jnp.int32)
    return (
        jnp.zeros((row_count, width_local), jnp.bfloat16)
        .at[arrived_places.reshape(-1)]
        .set(arrived_rows.reshape(row_count, width_local))
    )


def solution(mesh):
    placed = (
        P("wide", "narrow"),
        P("narrow", None),
        P("wide", "narrow"),
        P(),
        P("wide", None),
        P("wide", None),
        P("wide"),
        P(),
        P("wide", None, "narrow", None),
        P("wide", "narrow", None),
    )
    return jax.shard_map(
        local, mesh=mesh, in_specs=placed, out_specs=P("wide", "narrow"), check_vma=False
    )
```

```python
import jax
import jax.numpy as jnp
from jax import lax
from jax.sharding import PartitionSpec as P

EXPERTS = 32
CAP = 32


def running_rank(onehot):
    return jnp.sum((jnp.cumsum(onehot, axis=0) - onehot) * onehot, axis=1)


def local(
    attn_heads,
    w_out,
    residual,
    norm_gain,
    route_ids,
    route_weight,
    row_order,
    slot_expert,
    w_in,
    w_down,
):
    row_count = residual.shape[0]
    wide_count = lax.axis_size("wide")
    narrow_count = lax.axis_size("narrow")
    width_local = residual.shape[1]
    model_width = width_local * narrow_count
    me_narrow = lax.axis_index("narrow")

    slot_local = w_in.shape[0]
    hid_local = w_down.shape[1]
    w_in_all = lax.all_gather(w_in, "narrow", axis=0, tiled=False)
    shifted = [w_down] + [
        lax.ppermute(
            w_down,
            "narrow",
            perm=[(i, (i + k) % narrow_count) for i in range(narrow_count)],
        )
        for k in range(1, narrow_count)
    ]
    from_shift = (me_narrow - jnp.arange(narrow_count, dtype=jnp.int32)) % narrow_count
    w_down_all = jnp.take(jnp.stack(shifted), from_shift, axis=0)

    partial_terms = jnp.dot(attn_heads, w_out, preferred_element_type=jnp.float32)
    partial_terms = jnp.broadcast_to(
        partial_terms.astype(jnp.bfloat16)[None], (narrow_count, row_count, model_width)
    )
    partial_terms = lax.all_to_all(partial_terms, "narrow", split_axis=0, concat_axis=0, tiled=True)
    projected = jnp.sum(partial_terms.astype(jnp.float32), axis=0)
    spread = jnp.broadcast_to(residual[None], (narrow_count, row_count, width_local))
    spread = lax.all_to_all(spread, "narrow", split_axis=0, concat_axis=0, tiled=True)
    residual_rows = jnp.moveaxis(spread, 0, 1).reshape(row_count, model_width)
    hidden_rows = (residual_rows.astype(jnp.float32) + projected).astype(jnp.bfloat16)
    hidden = lax.dynamic_slice_in_dim(hidden_rows, me_narrow * width_local, width_local, axis=1)
    hidden_f = hidden.astype(jnp.float32)
    whole_rows = hidden_rows.astype(jnp.float32)
    mean_sq = jnp.mean(whole_rows * whole_rows, axis=1, keepdims=True)
    normed = (whole_rows * lax.rsqrt(mean_sq + 1e-06) * norm_gain).astype(jnp.bfloat16)

    slot_count = slot_expert.shape[0]
    top_count = route_ids.shape[1]
    band = CAP // narrow_count
    held = (slot_expert[None, :] == jnp.arange(EXPERTS, dtype=jnp.int32)[:, None]).astype(jnp.int32)
    copies = jnp.sum(held, axis=1)
    replica_rank = jnp.cumsum(held, axis=1) - held
    flat_ids = route_ids.reshape(-1)
    choose_expert = (flat_ids[:, None] == jnp.arange(EXPERTS, dtype=jnp.int32)[None, :]).astype(
        jnp.int32
    )
    copy_count = jnp.sum(choose_expert * copies[None, :], axis=1)
    replica = jnp.repeat(row_order, top_count) % copy_count
    held_rows = jnp.sum(choose_expert[:, :, None] * held[None, :, :], axis=1)
    rank_rows = jnp.sum(choose_expert[:, :, None] * replica_rank[None, :, :], axis=1)
    slot_hit = held_rows * (rank_rows == replica[:, None]).astype(jnp.int32)
    slot_index = jnp.sum(slot_hit * jnp.arange(slot_count, dtype=jnp.int32)[None, :], axis=1)
    rank = running_rank(slot_hit)
    position = slot_index * CAP + rank
    send_at = jnp.where(
        rank // band == me_narrow, slot_index * band + rank % band, slot_count * band
    )
    picks = send_at.reshape(row_count, top_count)[None, :, :] == jnp.arange(
        slot_count * band, dtype=jnp.int32
    )[:, None, None]
    picks = jnp.any(picks, axis=2).astype(jnp.bfloat16)
    outgoing = jnp.dot(picks, normed, preferred_element_type=jnp.float32).astype(jnp.bfloat16)
    outgoing = outgoing.reshape(wide_count, slot_local, band, model_width)
    arrived = lax.all_to_all(outgoing, "wide", split_axis=0, concat_axis=0, tiled=True)
    gate_up = jnp.einsum(
        "nscd,qsghd->nscgqh", arrived, w_in_all, preferred_element_type=jnp.float32
    )
    active = (jax.nn.relu(gate_up[:, :, :, 0]) * gate_up[:, :, :, 1]).astype(jnp.bfloat16)
    w_down_cols = w_down_all.reshape(
        narrow_count, slot_local, hid_local, narrow_count, width_local
    )
    lowered = jnp.einsum(
        "nscqh,qshpd->qnpscd", active, w_down_cols, preferred_element_type=jnp.float32
    )
    pieces = lowered.astype(jnp.bfloat16).astype(jnp.float32)
    summed = jnp.sum(pieces, axis=0).astype(jnp.bfloat16)
    summed = summed.reshape(wide_count * narrow_count, slot_local, band, width_local)
    returned = lax.all_to_all(
        summed, ("wide", "narrow"), split_axis=0, concat_axis=0, tiled=True
    )
    returned = returned.reshape(wide_count, narrow_count, slot_local, band, width_local)
    returned = jnp.swapaxes(returned, 1, 2)
    expert_out = returned.reshape(slot_count * CAP, width_local)[position]
    weighted = route_weight[:, :, None] * expert_out.reshape(
        row_count, top_count, width_local
    ).astype(jnp.float32)
    mixed = (hidden_f + jnp.sum(weighted, axis=1)).astype(jnp.bfloat16)
    pair_rows = row_count // wide_count
    target_dev = row_order // row_count
    target_place = row_order % row_count
    choose_target = (
        target_dev[:, None] == jnp.arange(wide_count, dtype=jnp.int32)[None, :]
    ).astype(jnp.int32)
    packed_index = target_dev * pair_rows + running_rank(choose_target)
    packed = jnp.zeros((row_count, width_local), jnp.bfloat16).at[packed_index].set(mixed)
    places = jnp.zeros((row_count,), jnp.int32).at[packed_index].set(target_place)
    assert row_count <= 256 and pair_rows <= width_local
    place_row = jnp.zeros((wide_count, 1, width_local), jnp.bfloat16)
    place_row = place_row.at[:, 0, :pair_rows].set(
        places.reshape(wide_count, pair_rows).astype(jnp.bfloat16)
    )
    packed = jnp.concatenate(
        [packed.reshape(wide_count, pair_rows, width_local), place_row], axis=1
    )
    arrived_all = lax.all_to_all(packed, "wide", split_axis=0, concat_axis=0, tiled=True)
    arrived_rows = arrived_all[:, :pair_rows]
    arrived_places = arrived_all[:, pair_rows, :pair_rows].astype(jnp.int32)
    return (
        jnp.zeros((row_count, width_local), jnp.bfloat16)
        .at[arrived_places.reshape(-1)]
        .set(arrived_rows.reshape(row_count, width_local))
    )


def solution(mesh):
    placed = (
        P("wide", "narrow"),
        P("narrow", None),
        P("wide", "narrow"),
        P(),
        P("wide", None),
        P("wide", None),
        P("wide"),
        P(),
        P("wide", None, "narrow", None),
        P("wide", "narrow", None),
    )
    return jax.shard_map(
        local, mesh=mesh, in_specs=placed, out_specs=P("wide", "narrow"), check_vma=False
    )
```

```python
import jax
import jax.numpy as jnp
from jax import lax
from jax.sharding import PartitionSpec as P


EXPERTS = 32
CAP = 32


def running_rank(onehot):
    return jnp.sum((jnp.cumsum(onehot, axis=0) - onehot) * onehot, axis=1)


def block(
    attn_heads,
    w_out,
    residual,
    norm_gain,
    route_ids,
    route_weight,
    row_order,
    slot_expert,
    w_in,
    w_down,
):
    row_count = residual.shape[0]
    wide_count = lax.axis_size("wide")
    narrow_count = lax.axis_size("narrow")
    width_local = residual.shape[1]
    model_width = width_local * narrow_count
    me_narrow = lax.axis_index("narrow")

    slot_local = w_in.shape[0]
    def ring(weights):
        return jnp.stack(
            [weights]
            + [
                lax.ppermute(
                    weights,
                    "narrow",
                    perm=[(i, (i + k) % narrow_count) for i in range(narrow_count)],
                )
                for k in range(1, narrow_count)
            ]
        )

    hid_local = w_down.shape[1]
    w_in_all = ring(w_in)
    w_down_all = ring(w_down)

    partial_terms = jnp.dot(attn_heads, w_out, preferred_element_type=jnp.float32)
    partial_terms = partial_terms.astype(jnp.bfloat16).reshape(
        row_count, narrow_count, width_local
    )
    partial_terms = jnp.swapaxes(partial_terms, 0, 1)
    partial_terms = lax.all_to_all(partial_terms, "narrow", split_axis=0, concat_axis=0, tiled=True)
    projected = jnp.sum(partial_terms.astype(jnp.float32), axis=0)
    hidden = (residual.astype(jnp.float32) + projected).astype(jnp.bfloat16)
    hidden_f = hidden.astype(jnp.float32)
    spread = jnp.broadcast_to(hidden[None], (narrow_count, row_count, width_local))
    spread = lax.all_to_all(spread, "narrow", split_axis=0, concat_axis=0, tiled=True)
    whole_rows = jnp.moveaxis(spread, 0, 1).reshape(row_count, model_width)
    whole_rows = whole_rows.astype(jnp.float32)
    mean_sq = jnp.mean(whole_rows * whole_rows, axis=1, keepdims=True)
    normed = (whole_rows * lax.rsqrt(mean_sq + 1e-06) * norm_gain).astype(jnp.bfloat16)

    slot_count = slot_expert.shape[0]
    top_count = route_ids.shape[1]
    band = CAP // narrow_count
    held = (slot_expert[None, :] == jnp.arange(EXPERTS, dtype=jnp.int32)[:, None]).astype(jnp.int32)
    copies = jnp.sum(held, axis=1)
    replica_rank = jnp.cumsum(held, axis=1) - held
    flat_ids = route_ids.reshape(-1)
    choose_expert = (flat_ids[:, None] == jnp.arange(EXPERTS, dtype=jnp.int32)[None, :]).astype(
        jnp.int32
    )
    copy_count = jnp.sum(choose_expert * copies[None, :], axis=1)
    replica = jnp.repeat(row_order, top_count) % copy_count
    held_rows = jnp.sum(choose_expert[:, :, None] * held[None, :, :], axis=1)
    rank_rows = jnp.sum(choose_expert[:, :, None] * replica_rank[None, :, :], axis=1)
    slot_hit = held_rows * (rank_rows == replica[:, None]).astype(jnp.int32)
    slot_index = jnp.sum(slot_hit * jnp.arange(slot_count, dtype=jnp.int32)[None, :], axis=1)
    rank = running_rank(slot_hit)
    position = slot_index * CAP + rank
    send_at = jnp.where(
        rank // band == me_narrow, slot_index * band + rank % band, slot_count * band
    )
    picks = send_at.reshape(row_count, top_count)[None, :, :] == jnp.arange(
        slot_count * band, dtype=jnp.int32
    )[:, None, None]
    picks = jnp.any(picks, axis=2).astype(jnp.bfloat16)
    outgoing = jnp.dot(picks, normed, preferred_element_type=jnp.float32).astype(jnp.bfloat16)
    outgoing = outgoing.reshape(wide_count, slot_local, band, model_width)
    arrived = lax.all_to_all(outgoing, "wide", split_axis=0, concat_axis=0, tiled=True)
    gate_up = jnp.einsum(
        "nscd,qsghd->nscgqh", arrived, w_in_all, preferred_element_type=jnp.float32
    )
    active = (jax.nn.relu(gate_up[:, :, :, 0]) * gate_up[:, :, :, 1]).astype(jnp.bfloat16)
    w_down_cols = w_down_all.reshape(
        narrow_count, slot_local, hid_local, narrow_count, width_local
    )
    lowered = jnp.einsum(
        "nscqh,qshpd->qnpscd", active, w_down_cols, preferred_element_type=jnp.float32
    )
    pieces = lowered.astype(jnp.bfloat16).astype(jnp.float32)
    summed = jnp.sum(pieces, axis=0).astype(jnp.bfloat16)
    summed = summed.reshape(wide_count * narrow_count, slot_local, band, width_local)
    returned = lax.all_to_all(
        summed, ("wide", "narrow"), split_axis=0, concat_axis=0, tiled=True
    )
    returned = returned.reshape(wide_count, narrow_count, slot_local, band, width_local)
    returned = jnp.swapaxes(returned, 1, 2)
    expert_out = returned.reshape(slot_count * CAP, width_local)[position]
    weighted = route_weight[:, :, None] * expert_out.reshape(
        row_count, top_count, width_local
    ).astype(jnp.float32)
    mixed = (hidden_f + jnp.sum(weighted, axis=1)).astype(jnp.bfloat16)
    pair_rows = row_count // wide_count
    target_dev = row_order // row_count
    target_place = row_order % row_count
    choose_target = (
        target_dev[:, None] == jnp.arange(wide_count, dtype=jnp.int32)[None, :]
    ).astype(jnp.int32)
    packed_index = target_dev * pair_rows + running_rank(choose_target)
    packed = jnp.zeros((row_count, width_local), jnp.bfloat16).at[packed_index].set(mixed)
    places = jnp.zeros((row_count,), jnp.int32).at[packed_index].set(target_place)
    assert row_count <= 256 and pair_rows <= width_local
    place_row = jnp.zeros((wide_count, 1, width_local), jnp.bfloat16)
    place_row = place_row.at[:, 0, :pair_rows].set(
        places.reshape(wide_count, pair_rows).astype(jnp.bfloat16)
    )
    packed = jnp.concatenate(
        [packed.reshape(wide_count, pair_rows, width_local), place_row], axis=1
    )
    arrived_all = lax.all_to_all(packed, "wide", split_axis=0, concat_axis=0, tiled=True)
    arrived_rows = arrived_all[:, :pair_rows]
    arrived_places = arrived_all[:, pair_rows, :pair_rows].astype(jnp.int32)
    return (
        jnp.zeros((row_count, width_local), jnp.bfloat16)
        .at[arrived_places.reshape(-1)]
        .set(arrived_rows.reshape(row_count, width_local))
    )


def solution(mesh):
    placed = (
        P("wide", "narrow"),
        P("narrow", None),
        P("wide", "narrow"),
        P(),
        P("wide", None),
        P("wide", None),
        P("wide"),
        P(),
        P("wide", None, "narrow", None),
        P("wide", "narrow", None),
    )
    return jax.shard_map(
        block, mesh=mesh, in_specs=placed, out_specs=P("wide", "narrow"), check_vma=False
    )
```

```python
import jax
import jax.numpy as jnp
from jax import lax
from jax.sharding import PartitionSpec as P


EXPERTS = 32
CAP = 32


def running_rank(onehot):
    return jnp.sum((jnp.cumsum(onehot, axis=0) - onehot) * onehot, axis=1)


def block(
    attn_heads,
    w_out,
    residual,
    norm_gain,
    route_ids,
    route_weight,
    row_order,
    slot_expert,
    w_in,
    w_down,
):
    row_count = residual.shape[0]
    wide_count = lax.axis_size("wide")
    narrow_count = lax.axis_size("narrow")
    width_local = residual.shape[1]
    model_width = width_local * narrow_count
    me_narrow = lax.axis_index("narrow")

    slot_local = w_in.shape[0]
    def ring(weights):
        return [weights] + [
            lax.ppermute(
                weights,
                "narrow",
                perm=[(i, (i + k) % narrow_count) for i in range(narrow_count)],
            )
            for k in range(1, narrow_count)
        ]

    w_in_all = ring(w_in)
    w_down_all = ring(w_down)

    partial_terms = jnp.dot(attn_heads, w_out, preferred_element_type=jnp.float32)
    partial_terms = partial_terms.astype(jnp.bfloat16).reshape(
        row_count, narrow_count, width_local
    )
    partial_terms = jnp.swapaxes(partial_terms, 0, 1)
    partial_terms = lax.all_to_all(partial_terms, "narrow", split_axis=0, concat_axis=0, tiled=True)
    projected = jnp.sum(partial_terms.astype(jnp.float32), axis=0)
    hidden = (residual.astype(jnp.float32) + projected).astype(jnp.bfloat16)
    hidden_f = hidden.astype(jnp.float32)
    spread = jnp.broadcast_to(hidden[None], (narrow_count, row_count, width_local))
    spread = lax.all_to_all(spread, "narrow", split_axis=0, concat_axis=0, tiled=True)
    whole_rows = jnp.moveaxis(spread, 0, 1).reshape(row_count, model_width)
    whole_rows = whole_rows.astype(jnp.float32)
    mean_sq = jnp.mean(whole_rows * whole_rows, axis=1, keepdims=True)
    normed = (whole_rows * lax.rsqrt(mean_sq + 1e-06) * norm_gain).astype(jnp.bfloat16)

    slot_count = slot_expert.shape[0]
    top_count = route_ids.shape[1]
    band = CAP // narrow_count
    held = (slot_expert[None, :] == jnp.arange(EXPERTS, dtype=jnp.int32)[:, None]).astype(jnp.int32)
    copies = jnp.sum(held, axis=1)
    replica_rank = jnp.cumsum(held, axis=1) - held
    flat_ids = route_ids.reshape(-1)
    choose_expert = (flat_ids[:, None] == jnp.arange(EXPERTS, dtype=jnp.int32)[None, :]).astype(
        jnp.int32
    )
    copy_count = jnp.sum(choose_expert * copies[None, :], axis=1)
    replica = jnp.repeat(row_order, top_count) % copy_count
    held_rows = jnp.sum(choose_expert[:, :, None] * held[None, :, :], axis=1)
    rank_rows = jnp.sum(choose_expert[:, :, None] * replica_rank[None, :, :], axis=1)
    slot_hit = held_rows * (rank_rows == replica[:, None]).astype(jnp.int32)
    slot_index = jnp.sum(slot_hit * jnp.arange(slot_count, dtype=jnp.int32)[None, :], axis=1)
    rank = running_rank(slot_hit)
    position = slot_index * CAP + rank
    send_at = jnp.where(
        rank // band == me_narrow, slot_index * band + rank % band, slot_count * band
    )
    picks = send_at.reshape(row_count, top_count)[None, :, :] == jnp.arange(
        slot_count * band, dtype=jnp.int32
    )[:, None, None]
    picks = jnp.any(picks, axis=2).astype(jnp.bfloat16)
    outgoing = jnp.dot(picks, normed, preferred_element_type=jnp.float32).astype(jnp.bfloat16)
    outgoing = outgoing.reshape(wide_count, slot_local, band, model_width)
    arrived = lax.all_to_all(outgoing, "wide", split_axis=0, concat_axis=0, tiled=True)
    summed = None
    for w_in_k, w_down_k in zip(w_in_all, w_down_all):
        gate_up = jnp.einsum(
            "nscd,sghd->nscgh", arrived, w_in_k, preferred_element_type=jnp.float32
        )
        active = (jax.nn.relu(gate_up[:, :, :, 0]) * gate_up[:, :, :, 1]).astype(jnp.bfloat16)
        piece = jnp.einsum(
            "nsch,shd->nscd", active, w_down_k, preferred_element_type=jnp.float32
        )
        piece = piece.astype(jnp.bfloat16).astype(jnp.float32)
        summed = piece if summed is None else summed + piece
    summed = summed.astype(jnp.bfloat16).reshape(
        wide_count, slot_local, band, narrow_count, width_local
    )
    summed = jnp.moveaxis(summed, 3, 1)
    summed = summed.reshape(wide_count * narrow_count, slot_local, band, width_local)
    returned = lax.all_to_all(
        summed, ("wide", "narrow"), split_axis=0, concat_axis=0, tiled=True
    )
    returned = returned.reshape(wide_count, narrow_count, slot_local, band, width_local)
    returned = jnp.swapaxes(returned, 1, 2)
    expert_out = returned.reshape(slot_count * CAP, width_local)[position]
    weighted = route_weight[:, :, None] * expert_out.reshape(
        row_count, top_count, width_local
    ).astype(jnp.float32)
    mixed = (hidden_f + jnp.sum(weighted, axis=1)).astype(jnp.bfloat16)
    pair_rows = row_count // wide_count
    target_dev = row_order // row_count
    target_place = row_order % row_count
    choose_target = (
        target_dev[:, None] == jnp.arange(wide_count, dtype=jnp.int32)[None, :]
    ).astype(jnp.int32)
    packed_index = target_dev * pair_rows + running_rank(choose_target)
    packed = jnp.zeros((row_count, width_local), jnp.bfloat16).at[packed_index].set(mixed)
    places = jnp.zeros((row_count,), jnp.int32).at[packed_index].set(target_place)
    assert row_count <= 256 and pair_rows <= width_local
    place_row = jnp.zeros((wide_count, 1, width_local), jnp.bfloat16)
    place_row = place_row.at[:, 0, :pair_rows].set(
        places.reshape(wide_count, pair_rows).astype(jnp.bfloat16)
    )
    packed = jnp.concatenate(
        [packed.reshape(wide_count, pair_rows, width_local), place_row], axis=1
    )
    arrived_all = lax.all_to_all(packed, "wide", split_axis=0, concat_axis=0, tiled=True)
    arrived_rows = arrived_all[:, :pair_rows]
    arrived_places = arrived_all[:, pair_rows, :pair_rows].astype(jnp.int32)
    return (
        jnp.zeros((row_count, width_local), jnp.bfloat16)
        .at[arrived_places.reshape(-1)]
        .set(arrived_rows.reshape(row_count, width_local))
    )


def solution(mesh):
    placed = (
        P("wide", "narrow"),
        P("narrow", None),
        P("wide", "narrow"),
        P(),
        P("wide", None),
        P("wide", None),
        P("wide"),
        P(),
        P("wide", None, "narrow", None),
        P("wide", "narrow", None),
    )
    return jax.shard_map(
        block, mesh=mesh, in_specs=placed, out_specs=P("wide", "narrow"), check_vma=False
    )
```

```python
import jax
import jax.numpy as jnp
from jax import lax
from jax.sharding import PartitionSpec as P


EXPERTS = 32
CAP = 32


def running_rank(onehot):
    return jnp.sum((jnp.cumsum(onehot, axis=0) - onehot) * onehot, axis=1)


def block(
    attn_heads,
    w_out,
    residual,
    norm_gain,
    route_ids,
    route_weight,
    row_order,
    slot_expert,
    w_in,
    w_down,
):
    row_count = residual.shape[0]
    wide_count = lax.axis_size("wide")
    narrow_count = lax.axis_size("narrow")
    width_local = residual.shape[1]
    model_width = width_local * narrow_count
    me_narrow = lax.axis_index("narrow")

    slot_local = w_in.shape[0]
    def ring(weights):
        return [weights] + [
            lax.ppermute(
                weights,
                "narrow",
                perm=[(i, (i + k) % narrow_count) for i in range(narrow_count)],
            )
            for k in range(1, narrow_count)
        ]

    w_in_all = ring(w_in)
    w_down_all = ring(w_down)

    partial_terms = jnp.dot(attn_heads, w_out, preferred_element_type=jnp.float32)
    partial_terms = partial_terms.astype(jnp.bfloat16).reshape(
        row_count, narrow_count, width_local
    )
    partial_terms = jnp.swapaxes(partial_terms, 0, 1)
    partial_terms = lax.all_to_all(partial_terms, "narrow", split_axis=0, concat_axis=0, tiled=True)
    projected = jnp.sum(partial_terms.astype(jnp.float32), axis=0)
    hidden = (residual.astype(jnp.float32) + projected).astype(jnp.bfloat16)
    hidden_f = hidden.astype(jnp.float32)
    spread = jnp.broadcast_to(hidden[None], (narrow_count, row_count, width_local))
    spread = lax.all_to_all(spread, "narrow", split_axis=0, concat_axis=0, tiled=True)
    whole_rows = jnp.moveaxis(spread, 0, 1).reshape(row_count, model_width)
    whole_rows = whole_rows.astype(jnp.float32)
    mean_sq = jnp.mean(whole_rows * whole_rows, axis=1, keepdims=True)
    normed = (whole_rows * lax.rsqrt(mean_sq + 1e-06) * norm_gain).astype(jnp.bfloat16)

    slot_count = slot_expert.shape[0]
    top_count = route_ids.shape[1]
    band = CAP // narrow_count
    held = (slot_expert[None, :] == jnp.arange(EXPERTS, dtype=jnp.int32)[:, None]).astype(jnp.int32)
    copies = jnp.sum(held, axis=1)
    replica_rank = jnp.cumsum(held, axis=1) - held
    flat_ids = route_ids.reshape(-1)
    choose_expert = (flat_ids[:, None] == jnp.arange(EXPERTS, dtype=jnp.int32)[None, :]).astype(
        jnp.int32
    )
    copy_count = jnp.sum(choose_expert * copies[None, :], axis=1)
    replica = jnp.repeat(row_order, top_count) % copy_count
    held_rows = jnp.sum(choose_expert[:, :, None] * held[None, :, :], axis=1)
    rank_rows = jnp.sum(choose_expert[:, :, None] * replica_rank[None, :, :], axis=1)
    slot_hit = held_rows * (rank_rows == replica[:, None]).astype(jnp.int32)
    slot_index = jnp.sum(slot_hit * jnp.arange(slot_count, dtype=jnp.int32)[None, :], axis=1)
    rank = running_rank(slot_hit)
    position = slot_index * CAP + rank
    send_at = jnp.where(
        rank // band == me_narrow, slot_index * band + rank % band, slot_count * band
    )
    picks = send_at.reshape(row_count, top_count)[None, :, :] == jnp.arange(
        slot_count * band, dtype=jnp.int32
    )[:, None, None]
    picks = jnp.any(picks, axis=2).astype(jnp.bfloat16)
    outgoing = jnp.dot(picks, normed, preferred_element_type=jnp.float32).astype(jnp.bfloat16)
    outgoing = outgoing.reshape(wide_count, slot_local, band, model_width)
    arrived = lax.all_to_all(outgoing, "wide", split_axis=0, concat_axis=0, tiled=True)
    summed = None
    for w_in_k, w_down_k in zip(w_in_all, w_down_all):
        gate_up = jnp.einsum(
            "nscd,sghd->nscgh", arrived, w_in_k, preferred_element_type=jnp.float32
        )
        active = (jax.nn.relu(gate_up[:, :, :, 0]) * gate_up[:, :, :, 1]).astype(jnp.bfloat16)
        piece = jnp.einsum(
            "nsch,shd->nscd", active, w_down_k, preferred_element_type=jnp.float32
        )
        piece = piece.astype(jnp.bfloat16).astype(jnp.float32)
        summed = piece if summed is None else summed + piece
    summed = summed.astype(jnp.bfloat16).reshape(
        wide_count, slot_local, band, narrow_count, width_local
    )
    summed = jnp.moveaxis(summed, 3, 1)
    summed = summed.reshape(wide_count * narrow_count, slot_local, band, width_local)
    returned = lax.all_to_all(
        summed, ("wide", "narrow"), split_axis=0, concat_axis=0, tiled=True
    )
    returned = returned.reshape(wide_count, narrow_count, slot_local, band, width_local)
    returned = jnp.swapaxes(returned, 1, 2)
    returned = returned.reshape(slot_count * CAP, width_local)
    take_rows = (
        position[:, None] == jnp.arange(slot_count * CAP, dtype=jnp.int32)[None, :]
    ).astype(jnp.bfloat16)
    expert_out = jnp.dot(take_rows, returned, preferred_element_type=jnp.float32)
    weighted = route_weight[:, :, None] * expert_out.reshape(
        row_count, top_count, width_local
    ).astype(jnp.float32)
    mixed = (hidden_f + jnp.sum(weighted, axis=1)).astype(jnp.bfloat16)
    pair_rows = row_count // wide_count
    target_dev = row_order // row_count
    target_place = row_order % row_count
    choose_target = (
        target_dev[:, None] == jnp.arange(wide_count, dtype=jnp.int32)[None, :]
    ).astype(jnp.int32)
    packed_index = target_dev * pair_rows + running_rank(choose_target)
    pack_rows = (
        packed_index[None, :] == jnp.arange(row_count, dtype=jnp.int32)[:, None]
    ).astype(jnp.bfloat16)
    packed = jnp.dot(pack_rows, mixed, preferred_element_type=jnp.float32).astype(jnp.bfloat16)
    places = jnp.zeros((row_count,), jnp.int32).at[packed_index].set(target_place)
    assert row_count <= 256 and pair_rows <= width_local
    place_row = jnp.zeros((wide_count, 1, width_local), jnp.bfloat16)
    place_row = place_row.at[:, 0, :pair_rows].set(
        places.reshape(wide_count, pair_rows).astype(jnp.bfloat16)
    )
    packed = jnp.concatenate(
        [packed.reshape(wide_count, pair_rows, width_local), place_row], axis=1
    )
    arrived_all = lax.all_to_all(packed, "wide", split_axis=0, concat_axis=0, tiled=True)
    arrived_rows = arrived_all[:, :pair_rows]
    arrived_places = arrived_all[:, pair_rows, :pair_rows].astype(jnp.int32)
    place_rows = (
        arrived_places.reshape(1, -1) == jnp.arange(row_count, dtype=jnp.int32)[:, None]
    ).astype(jnp.bfloat16)
    return jnp.dot(
        place_rows,
        arrived_rows.reshape(row_count, width_local),
        preferred_element_type=jnp.float32,
    ).astype(jnp.bfloat16)


def solution(mesh):
    placed = (
        P("wide", "narrow"),
        P("narrow", None),
        P("wide", "narrow"),
        P(),
        P("wide", None),
        P("wide", None),
        P("wide"),
        P(),
        P("wide", None, "narrow", None),
        P("wide", "narrow", None),
    )
    return jax.shard_map(
        block, mesh=mesh, in_specs=placed, out_specs=P("wide", "narrow"), check_vma=False
    )
```

```python
import jax
import jax.numpy as jnp
from jax import lax
from jax.sharding import PartitionSpec as P


EXPERTS = 32
CAP = 32


def running_rank(onehot):
    return jnp.sum((jnp.cumsum(onehot, axis=0) - onehot) * onehot, axis=1)


def block(
    attn_heads,
    w_out,
    residual,
    norm_gain,
    route_ids,
    route_weight,
    row_order,
    slot_expert,
    w_in,
    w_down,
):
    row_count = residual.shape[0]
    wide_count = lax.axis_size("wide")
    narrow_count = lax.axis_size("narrow")
    width_local = residual.shape[1]
    model_width = width_local * narrow_count
    me_narrow = lax.axis_index("narrow")

    slot_local = w_in.shape[0]
    def ring(weights):
        return [weights] + [
            lax.ppermute(
                weights,
                "narrow",
                perm=[(i, (i + k) % narrow_count) for i in range(narrow_count)],
            )
            for k in range(1, narrow_count)
        ]

    hid_local = w_down.shape[1]
    w_in_all = ring(w_in)
    w_down_all = ring(w_down)

    partial_terms = jnp.dot(attn_heads, w_out, preferred_element_type=jnp.float32)
    partial_terms = partial_terms.astype(jnp.bfloat16).reshape(
        row_count, narrow_count, width_local
    )
    partial_terms = jnp.swapaxes(partial_terms, 0, 1)
    partial_terms = lax.all_to_all(partial_terms, "narrow", split_axis=0, concat_axis=0, tiled=True)
    projected = jnp.sum(partial_terms.astype(jnp.float32), axis=0)
    hidden = (residual.astype(jnp.float32) + projected).astype(jnp.bfloat16)
    hidden_f = hidden.astype(jnp.float32)
    spread = jnp.broadcast_to(hidden[None], (narrow_count, row_count, width_local))
    spread = lax.all_to_all(spread, "narrow", split_axis=0, concat_axis=0, tiled=True)
    whole_rows = jnp.moveaxis(spread, 0, 1).reshape(row_count, model_width)
    whole_rows = whole_rows.astype(jnp.float32)
    mean_sq = jnp.mean(whole_rows * whole_rows, axis=1, keepdims=True)
    normed = (whole_rows * lax.rsqrt(mean_sq + 1e-06) * norm_gain).astype(jnp.bfloat16)

    slot_count = slot_expert.shape[0]
    top_count = route_ids.shape[1]
    band = CAP // narrow_count
    held = (slot_expert[None, :] == jnp.arange(EXPERTS, dtype=jnp.int32)[:, None]).astype(jnp.int32)
    copies = jnp.sum(held, axis=1)
    replica_rank = jnp.cumsum(held, axis=1) - held
    flat_ids = route_ids.reshape(-1)
    choose_expert = (flat_ids[:, None] == jnp.arange(EXPERTS, dtype=jnp.int32)[None, :]).astype(
        jnp.int32
    )
    copy_count = jnp.sum(choose_expert * copies[None, :], axis=1)
    replica = jnp.repeat(row_order, top_count) % copy_count
    held_rows = jnp.sum(choose_expert[:, :, None] * held[None, :, :], axis=1)
    rank_rows = jnp.sum(choose_expert[:, :, None] * replica_rank[None, :, :], axis=1)
    slot_hit = held_rows * (rank_rows == replica[:, None]).astype(jnp.int32)
    slot_index = jnp.sum(slot_hit * jnp.arange(slot_count, dtype=jnp.int32)[None, :], axis=1)
    rank = running_rank(slot_hit)
    position = slot_index * CAP + rank
    send_at = jnp.where(
        rank // band == me_narrow, slot_index * band + rank % band, slot_count * band
    )
    picks = send_at.reshape(row_count, top_count)[None, :, :] == jnp.arange(
        slot_count * band, dtype=jnp.int32
    )[:, None, None]
    picks = jnp.any(picks, axis=2).astype(jnp.bfloat16)
    outgoing = jnp.dot(picks, normed, preferred_element_type=jnp.float32).astype(jnp.bfloat16)
    outgoing = outgoing.reshape(wide_count, slot_local, band, model_width)
    arrived = lax.all_to_all(outgoing, "wide", split_axis=0, concat_axis=0, tiled=True)
    summed = None
    for w_in_k, w_down_k in zip(w_in_all, w_down_all):
        gate_up = jnp.einsum(
            "nscd,sghd->nscgh", arrived, w_in_k, preferred_element_type=jnp.float32
        )
        active = (jax.nn.relu(gate_up[:, :, :, 0]) * gate_up[:, :, :, 1]).astype(jnp.bfloat16)
        w_down_cols = w_down_k.reshape(slot_local, hid_local, narrow_count, width_local)
        piece = jnp.einsum(
            "nsch,shpd->npscd", active, w_down_cols, preferred_element_type=jnp.float32
        )
        piece = piece.astype(jnp.bfloat16).astype(jnp.float32)
        summed = piece if summed is None else summed + piece
    summed = summed.astype(jnp.bfloat16)
    summed = summed.reshape(wide_count * narrow_count, slot_local, band, width_local)
    returned = lax.all_to_all(
        summed, ("wide", "narrow"), split_axis=0, concat_axis=0, tiled=True
    )
    returned = returned.reshape(wide_count, narrow_count, slot_local, band, width_local)
    returned = jnp.swapaxes(returned, 1, 2)
    returned = returned.reshape(slot_count * CAP, width_local)
    take_rows = (
        position[:, None] == jnp.arange(slot_count * CAP, dtype=jnp.int32)[None, :]
    ).astype(jnp.bfloat16)
    expert_out = jnp.dot(take_rows, returned, preferred_element_type=jnp.float32)
    weighted = route_weight[:, :, None] * expert_out.reshape(
        row_count, top_count, width_local
    ).astype(jnp.float32)
    mixed = (hidden_f + jnp.sum(weighted, axis=1)).astype(jnp.bfloat16)
    pair_rows = row_count // wide_count
    target_dev = row_order // row_count
    target_place = row_order % row_count
    choose_target = (
        target_dev[:, None] == jnp.arange(wide_count, dtype=jnp.int32)[None, :]
    ).astype(jnp.int32)
    packed_index = target_dev * pair_rows + running_rank(choose_target)
    pack_rows = (
        packed_index[None, :] == jnp.arange(row_count, dtype=jnp.int32)[:, None]
    ).astype(jnp.bfloat16)
    packed = jnp.dot(pack_rows, mixed, preferred_element_type=jnp.float32).astype(jnp.bfloat16)
    places = jnp.zeros((row_count,), jnp.int32).at[packed_index].set(target_place)
    assert row_count <= 256 and pair_rows <= width_local
    place_row = jnp.zeros((wide_count, 1, width_local), jnp.bfloat16)
    place_row = place_row.at[:, 0, :pair_rows].set(
        places.reshape(wide_count, pair_rows).astype(jnp.bfloat16)
    )
    packed = jnp.concatenate(
        [packed.reshape(wide_count, pair_rows, width_local), place_row], axis=1
    )
    arrived_all = lax.all_to_all(packed, "wide", split_axis=0, concat_axis=0, tiled=True)
    arrived_rows = arrived_all[:, :pair_rows]
    arrived_places = arrived_all[:, pair_rows, :pair_rows].astype(jnp.int32)
    place_rows = (
        arrived_places.reshape(1, -1) == jnp.arange(row_count, dtype=jnp.int32)[:, None]
    ).astype(jnp.bfloat16)
    return jnp.dot(
        place_rows,
        arrived_rows.reshape(row_count, width_local),
        preferred_element_type=jnp.float32,
    ).astype(jnp.bfloat16)


def solution(mesh):
    placed = (
        P("wide", "narrow"),
        P("narrow", None),
        P("wide", "narrow"),
        P(),
        P("wide", None),
        P("wide", None),
        P("wide"),
        P(),
        P("wide", None, "narrow", None),
        P("wide", "narrow", None),
    )
    return jax.shard_map(
        block, mesh=mesh, in_specs=placed, out_specs=P("wide", "narrow"), check_vma=False
    )
```

```python
import jax
import jax.numpy as jnp
from jax import lax
from jax.sharding import PartitionSpec as P


EXPERTS = 32
CAP = 32


def running_rank(onehot):
    return jnp.sum((jnp.cumsum(onehot, axis=0) - onehot) * onehot, axis=1)


def block(
    attn_heads,
    w_out,
    residual,
    norm_gain,
    route_ids,
    route_weight,
    row_order,
    slot_expert,
    w_in,
    w_down,
):
    row_count = residual.shape[0]
    wide_count = lax.axis_size("wide")
    narrow_count = lax.axis_size("narrow")
    width_local = residual.shape[1]
    model_width = width_local * narrow_count
    me_narrow = lax.axis_index("narrow")

    slot_local = w_in.shape[0]
    def ring(weights):
        return [weights] + [
            lax.ppermute(
                weights,
                "narrow",
                perm=[(i, (i + k) % narrow_count) for i in range(narrow_count)],
            )
            for k in range(1, narrow_count)
        ]

    w_in_all = ring(w_in)
    w_down_all = ring(w_down)

    partial_terms = jnp.dot(attn_heads, w_out, preferred_element_type=jnp.float32)
    partial_terms = partial_terms.astype(jnp.bfloat16).reshape(
        row_count, narrow_count, width_local
    )
    partial_terms = jnp.swapaxes(partial_terms, 0, 1)
    partial_terms = lax.all_to_all(partial_terms, "narrow", split_axis=0, concat_axis=0, tiled=True)
    projected = jnp.sum(partial_terms.astype(jnp.float32), axis=0)
    hidden = (residual.astype(jnp.float32) + projected).astype(jnp.bfloat16)
    hidden_f = hidden.astype(jnp.float32)
    spread = jnp.broadcast_to(hidden[None], (narrow_count, row_count, width_local))
    spread = lax.all_to_all(spread, "narrow", split_axis=0, concat_axis=0, tiled=True)
    whole_rows = jnp.moveaxis(spread, 0, 1).reshape(row_count, model_width)
    whole_rows = whole_rows.astype(jnp.float32)
    mean_sq = jnp.mean(whole_rows * whole_rows, axis=1, keepdims=True)
    normed = (whole_rows * lax.rsqrt(mean_sq + 1e-06) * norm_gain).astype(jnp.bfloat16)

    slot_count = slot_expert.shape[0]
    top_count = route_ids.shape[1]
    band = CAP // narrow_count
    held = (slot_expert[None, :] == jnp.arange(EXPERTS, dtype=jnp.int32)[:, None]).astype(jnp.int32)
    copies = jnp.sum(held, axis=1)
    replica_rank = jnp.cumsum(held, axis=1) - held
    flat_ids = route_ids.reshape(-1)
    choose_expert = (flat_ids[:, None] == jnp.arange(EXPERTS, dtype=jnp.int32)[None, :]).astype(
        jnp.int32
    )
    copy_count = jnp.sum(choose_expert * copies[None, :], axis=1)
    replica = jnp.repeat(row_order, top_count) % copy_count
    held_rows = jnp.sum(choose_expert[:, :, None] * held[None, :, :], axis=1)
    rank_rows = jnp.sum(choose_expert[:, :, None] * replica_rank[None, :, :], axis=1)
    slot_hit = held_rows * (rank_rows == replica[:, None]).astype(jnp.int32)
    slot_index = jnp.sum(slot_hit * jnp.arange(slot_count, dtype=jnp.int32)[None, :], axis=1)
    rank = running_rank(slot_hit)
    position = slot_index * CAP + rank
    send_at = jnp.where(
        rank // band == me_narrow, slot_index * band + rank % band, slot_count * band
    )
    picks = send_at.reshape(row_count, top_count)[None, :, :] == jnp.arange(
        slot_count * band, dtype=jnp.int32
    )[:, None, None]
    picks = jnp.any(picks, axis=2).astype(jnp.bfloat16)
    outgoing = jnp.dot(picks, normed, preferred_element_type=jnp.float32).astype(jnp.bfloat16)
    outgoing = outgoing.reshape(wide_count, slot_local, band, model_width)
    arrived = lax.all_to_all(outgoing, "wide", split_axis=0, concat_axis=0, tiled=True)
    summed = None
    for w_in_k, w_down_k in zip(w_in_all, w_down_all):
        gate_up = jnp.einsum(
            "nscd,sghd->nscgh", arrived, w_in_k, preferred_element_type=jnp.float32
        )
        active = (jax.nn.relu(gate_up[:, :, :, 0]) * gate_up[:, :, :, 1]).astype(jnp.bfloat16)
        piece = jnp.einsum(
            "nsch,shd->nscd", active, w_down_k, preferred_element_type=jnp.float32
        )
        piece = piece.astype(jnp.bfloat16).astype(jnp.float32)
        summed = piece if summed is None else summed + piece
    summed = summed.astype(jnp.bfloat16).reshape(
        wide_count, slot_local, band, narrow_count, width_local
    )
    summed = jnp.moveaxis(summed, 3, 0)
    summed = summed.reshape(narrow_count * wide_count, slot_local, band, width_local)
    returned = lax.all_to_all(
        summed, ("narrow", "wide"), split_axis=0, concat_axis=0, tiled=True
    )
    returned = returned.reshape(slot_count * CAP, width_local)
    position = (rank // band) * (slot_count * band) + slot_index * band + rank % band
    take_rows = (
        position[:, None] == jnp.arange(slot_count * CAP, dtype=jnp.int32)[None, :]
    ).astype(jnp.bfloat16)
    expert_out = jnp.dot(take_rows, returned, preferred_element_type=jnp.float32)
    weighted = route_weight[:, :, None] * expert_out.reshape(
        row_count, top_count, width_local
    ).astype(jnp.float32)
    mixed = (hidden_f + jnp.sum(weighted, axis=1)).astype(jnp.bfloat16)
    pair_rows = row_count // wide_count
    target_dev = row_order // row_count
    target_place = row_order % row_count
    choose_target = (
        target_dev[:, None] == jnp.arange(wide_count, dtype=jnp.int32)[None, :]
    ).astype(jnp.int32)
    packed_index = target_dev * pair_rows + running_rank(choose_target)
    pack_rows = (
        packed_index[None, :] == jnp.arange(row_count, dtype=jnp.int32)[:, None]
    ).astype(jnp.bfloat16)
    packed = jnp.dot(pack_rows, mixed, preferred_element_type=jnp.float32).astype(jnp.bfloat16)
    places = jnp.zeros((row_count,), jnp.int32).at[packed_index].set(target_place)
    assert row_count <= 256 and pair_rows <= width_local
    place_row = jnp.zeros((wide_count, 1, width_local), jnp.bfloat16)
    place_row = place_row.at[:, 0, :pair_rows].set(
        places.reshape(wide_count, pair_rows).astype(jnp.bfloat16)
    )
    packed = jnp.concatenate(
        [packed.reshape(wide_count, pair_rows, width_local), place_row], axis=1
    )
    arrived_all = lax.all_to_all(packed, "wide", split_axis=0, concat_axis=0, tiled=True)
    arrived_rows = arrived_all[:, :pair_rows]
    arrived_places = arrived_all[:, pair_rows, :pair_rows].astype(jnp.int32)
    place_rows = (
        arrived_places.reshape(1, -1) == jnp.arange(row_count, dtype=jnp.int32)[:, None]
    ).astype(jnp.bfloat16)
    return jnp.dot(
        place_rows,
        arrived_rows.reshape(row_count, width_local),
        preferred_element_type=jnp.float32,
    ).astype(jnp.bfloat16)


def solution(mesh):
    placed = (
        P("wide", "narrow"),
        P("narrow", None),
        P("wide", "narrow"),
        P(),
        P("wide", None),
        P("wide", None),
        P("wide"),
        P(),
        P("wide", None, "narrow", None),
        P("wide", "narrow", None),
    )
    return jax.shard_map(
        block, mesh=mesh, in_specs=placed, out_specs=P("wide", "narrow"), check_vma=False
    )
```
